256 devices in a mesh: row: 8 (over y, core), col: 32 (over x, z).
Axes of the slice: x: 4, y: 4, z: 8, core: 2. Of those that a mesh axis runs over, the one named last changes fastest.
Arguments:
- tokens: bfloat16 [256, 512, 192], P('row', 'col'), may hold values from -6 to 6
- tissue: int32 [256, 512], P('row', 'col'), may hold values 0 or 1
- ln_gain: float32 [192], replicated, may hold values from 0.5 to 1.5
- in_weight: bfloat16 [192, 768], replicated, may hold values from -0.4375 to 0.4375
- conv_weight: bfloat16 [3, 3, 384], replicated, may hold values from -2 to 2
- conv_bias: float32 [384], replicated, may hold values from -3 to 3
- proj_weight: bfloat16 [4, 384, 44], replicated, may hold values from -0.3125 to 0.3125
- dt_weight: bfloat16 [4, 12, 384], replicated, may hold values from -1.75 to 1.75
- dt_bias: float32 [4, 384], replicated, may hold values from -4 to -1
- a_rate: float32 [4, 384, 16], replicated, may hold values from 0.001 to 1
- skip_d: float32 [4, 384], replicated, may hold values from 0.5 to 1.5
- out_gain: float32 [384], replicated, may hold values from 0.5 to 1.5
- out_weight: bfloat16 [384, 192], replicated, may hold values from -0.3125 to 0.3125
Outputs:
- result: bfloat16 [256, 512, 192], P('row', 'col')
The draws below stay inside these ranges and needn't reach their ends.
Inputs may be any that keep to these rules, and one draw needn't show every extreme that they name: 1 marks a tissue token, 0 a background token.
All inputs are finite; a program needn't handle non-finite values. No bound on the sum of `tissue` on one device may be relied on, other than what follows from the above.
Results may differ from the reference program's by a relative error of at most 0.0055.
Values may be sent and summed in bfloat16 or wider, within the bound.
No kernel may reach another device: no remote copies, remote signals or barrier semaphores. Data moves between devices by JAX's collectives and lax.ppermute only.
A program may use at most 256 MiB of HBM per device.

```python
import math
import jax
import jax.numpy as jnp
from jax import lax

D = 192
E = 384
NSTATE = 16
RANK = 12
HEIGHT = 256
WIDTH = 512


def plant(result, stream_key, least, high):
    index_at = [jax.random.randint(jax.random.fold_in(stream_key, axis), (), 0, length) for axis, length in enumerate(result.shape)]
    main_axis = result.shape.index(max(result.shape))
    next_to = index_at[:main_axis] + [(index_at[main_axis] + 1) % result.shape[main_axis]] + index_at[main_axis + 1:]
    return result.at[tuple(index_at)].set(least).at[tuple(next_to)].set(high)


def steps_of(key, dims, cuts, smallest, top_value):
    factor_of, own = 1.0, jax.random.fold_in(key, 6)
    for axis_at, blocks in cuts:
        heights = jnp.exp(jax.random.uniform(jax.random.fold_in(own, axis_at), (blocks,), jnp.float32, smallest / len(cuts), top_value / len(cuts)))
        factor_of = factor_of * jnp.repeat(heights, dims[axis_at] // blocks).reshape([-1 if axis == axis_at else 1 for axis in range(len(dims))])
    return factor_of


def scatter_about(rng, dims, deviation, limit, pieces=(), kind=jnp.bfloat16):
    drawn = deviation * jax.random.normal(rng, dims, jnp.float32)
    if pieces:
        drawn = drawn * steps_of(rng, dims, pieces, -0.22, 0.18)
    return jnp.clip(drawn, -limit, limit).astype(kind)


def setup_inputs(seed: int = 0) -> dict:
    seeds = jax.random.split(jax.random.key(seed), 14)
    tokens = scatter_about(seeds[0], (HEIGHT, WIDTH, D), 1.0, 6.0, ((0, 8), (1, 32)))
    tissue = plant((jax.random.randint(seeds[1], (HEIGHT, WIDTH), 0, 4) < 3).astype(jnp.int32), jax.random.fold_in(seeds[1], 1), 0, 1)
    ln_gain = jnp.clip(1.0 + 0.1 * jax.random.normal(seeds[2], (D,), jnp.float32), 0.5, 1.5)
    in_weight = scatter_about(seeds[3], (D, 2 * E), D ** -0.5, 0.4375)
    conv_weight = scatter_about(seeds[4], (3, 3, E), 9 ** -0.5, 2.0)
    conv_bias = scatter_about(seeds[5], (E,), 0.5, 3.0, (), jnp.float32)
    proj_weight = scatter_about(seeds[6], (4, E, RANK + 2 * NSTATE), E ** -0.5, 0.3125)
    dt_weight = scatter_about(seeds[7], (4, RANK, E), RANK ** -0.5, 1.75)
    dt_bias = jnp.clip(jax.random.uniform(seeds[8], (4, E), jnp.float32, -4.0, -1.0), -4.0, -1.0)
    a_rate = jnp.clip(jnp.exp(jax.random.uniform(seeds[9], (4, E, NSTATE), jnp.float32, math.log(0.001), math.log(1.0))), 0.001, 1.0)
    skip_d = jnp.clip(jax.random.uniform(seeds[10], (4, E), jnp.float32, 0.5, 1.5), 0.5, 1.5)
    out_gain = jnp.clip(1.0 + 0.1 * jax.random.normal(seeds[11], (E,), jnp.float32), 0.5, 1.5)
    out_weight = scatter_about(seeds[12], (E, D), E ** -0.5, 0.3125)
    return {"tokens": tokens, "tissue": tissue, "ln_gain": ln_gain, "in_weight": in_weight, "conv_weight": conv_weight, "conv_bias": conv_bias, "proj_weight": proj_weight, "dt_weight": dt_weight, "dt_bias": dt_bias, "a_rate": a_rate, "skip_d": skip_d, "out_gain": out_gain, "out_weight": out_weight}


def layer_norm(values, gain):
    center = values - lax.optimization_barrier(jnp.mean(values, axis=-1, keepdims=True))
    spread = lax.optimization_barrier(jnp.mean(center * center, axis=-1, keepdims=True))
    return center * lax.rsqrt(spread + 1e-05) * gain

def conv_silu(padded, conv_weight, conv_bias, height, width):
    summed = jnp.broadcast_to(conv_bias.astype(jnp.float32), (height, width, conv_bias.shape[0]))
    for offset_row in range(3):
        for offset_col in range(3):
            window = padded[offset_row:offset_row + height, offset_col:offset_col + width]
            summed = summed + window.astype(jnp.float32) * conv_weight[offset_row, offset_col].astype(jnp.float32)
    return jax.nn.silu(summed).astype(jnp.bfloat16)

def direction_inputs(conv_out, tissue_wide, proj_one, dtw_one, dtb_one):
    rank = dtw_one.shape[0]
    nstate = (proj_one.shape[1] - rank) // 2
    rows, cols, inner = conv_out.shape
    flat = conv_out.reshape(rows * cols, inner)
    projections = jnp.dot(flat, proj_one, preferred_element_type=jnp.float32)
    rate_low = projections[:, :rank].astype(jnp.bfloat16)
    delta = jax.nn.softplus(jnp.dot(rate_low, dtw_one, preferred_element_type=jnp.float32) + dtb_one)
    delta = delta.reshape(rows, cols, inner) * tissue_wide[:, :, None]
    entry = projections[:, rank:rank + nstate].reshape(rows, cols, nstate)
    readout = projections[:, rank + nstate:].reshape(rows, cols, nstate)
    return (delta, entry, readout)

def to_seq(array, axis, flip):
    moved = jnp.moveaxis(array, axis, 0)
    if flip:
        moved = moved[::-1]
    return moved

def from_seq(array, axis, flip):
    if flip:
        array = array[::-1]
    return jnp.moveaxis(array, 0, axis)

def scan_steps(conv_seq, delta_seq, entry_seq, readout_seq, rates, skip_gain, initial):

    def advance(state, inputs):
        conv_now, delta_now, entry_now, readout_now = inputs
        conv_wide = conv_now.astype(jnp.float32)
        state = jnp.exp(-delta_now[:, :, None] * rates) * state + (delta_now * conv_wide)[:, :, None] * entry_now[:, None, :]
        output = lax.optimization_barrier(jnp.sum(state * readout_now[:, None, :], axis=2)) + skip_gain * conv_wide
        return (state, output)
    _, outputs = lax.scan(advance, initial, (conv_seq, delta_seq, entry_seq, readout_seq))
    return outputs

def run_local(conv_out, inputs, rates, skip_gain, axis, flip):
    delta, entry, readout = inputs
    conv_seq = to_seq(conv_out, axis, flip)
    initial = jnp.zeros((conv_seq.shape[1], rates.shape[0], rates.shape[1]), jnp.float32)
    outputs = scan_steps(conv_seq, to_seq(delta, axis, flip), to_seq(entry, axis, flip), to_seq(readout, axis, flip), rates, skip_gain, initial)
    return from_seq(outputs, axis, flip)

def reference(tokens, tissue, ln_gain, in_weight, conv_weight, conv_bias, proj_weight, dt_weight, dt_bias, a_rate, skip_d, out_gain, out_weight):
    height, width_cols, width = tokens.shape
    inner = in_weight.shape[1] // 2
    normed = layer_norm(tokens.astype(jnp.float32), ln_gain).astype(jnp.bfloat16)
    projected = jnp.dot(normed.reshape(height * width_cols, width), in_weight, preferred_element_type=jnp.float32)
    projected = projected.astype(jnp.bfloat16).reshape(height, width_cols, 2 * inner)
    inner_part = projected[:, :, :inner]
    gate_part = projected[:, :, inner:]
    padded = jnp.pad(inner_part, ((1, 1), (1, 1), (0, 0)))
    conv_out = conv_silu(padded, conv_weight, conv_bias, height, width_cols)
    tissue_wide = tissue.astype(jnp.float32)
    mixed_sum = jnp.zeros((height, width_cols, inner), jnp.float32)
    for direction in range(4):
        axis = 1 if direction % 2 == 0 else 0
        flip = direction >= 2
        inputs = direction_inputs(conv_out, tissue_wide, proj_weight[direction], dt_weight[direction], dt_bias[direction])
        mixed_sum = mixed_sum + run_local(conv_out, inputs, a_rate[direction], skip_d[direction], axis, flip)
    mixed = (layer_norm(mixed_sum, out_gain) * jax.nn.silu(gate_part.astype(jnp.float32))).astype(jnp.bfloat16)
    branch = jnp.dot(mixed.reshape(height * width_cols, inner), out_weight, preferred_element_type=jnp.float32)
    branch = branch.reshape(height, width_cols, width)
    return (tokens.astype(jnp.float32) + tissue_wide[:, :, None] * branch).astype(jnp.bfloat16)
```

```python
import functools

import jax
import jax.numpy as jnp
from jax import lax
from jax.experimental import pallas as pl
from jax.sharding import PartitionSpec as P


def padded_2(block, sides, width):
    for axis, dim in sides:
        count = lax.axis_size(axis)
        forward = [(i, i + 1) for i in range(count - 1)]
        backward = [(target, source) for source, target in forward]
        low = lax.ppermute(
            lax.slice_in_dim(block, block.shape[dim] - width, None, axis=dim), axis, forward
        )
        high = lax.ppermute(lax.slice_in_dim(block, 0, width, axis=dim), axis, backward)
        block = jnp.concatenate([low, block, high], axis=dim)
    return block


def layer_norm(values, gain):
    center = values - jnp.mean(values, axis=-1, keepdims=True)
    spread = jnp.mean(center * center, axis=-1, keepdims=True)
    return center * lax.rsqrt(spread + 1e-05) * gain


def conv_silu(padded, conv_weight, conv_bias, height, width):
    summed = jnp.broadcast_to(conv_bias, (height, width, conv_bias.shape[0]))
    for offset_row in range(3):
        for offset_col in range(3):
            window = padded[offset_row : offset_row + height, offset_col : offset_col + width]
            summed = summed + window.astype(jnp.float32) * conv_weight[
                offset_row, offset_col
            ].astype(jnp.float32)
    return jax.nn.silu(summed).astype(jnp.bfloat16)


def direction_inputs(seq_x, seq_mask, proj_one, dtw_one, dtb_one):
    rank = dtw_one.shape[0]
    nstate = (proj_one.shape[1] - rank) // 2
    length, seqs, inner = seq_x.shape
    flat = seq_x.reshape(length * seqs, inner)
    projections = jnp.dot(flat, proj_one, preferred_element_type=jnp.float32)
    rate_low = projections[:, :rank].astype(jnp.bfloat16)
    delta = jax.nn.softplus(
        jnp.dot(rate_low, dtw_one, preferred_element_type=jnp.float32) + dtb_one
    )
    delta = delta.reshape(length, seqs, inner) * seq_mask[:, :, None]
    entry = projections[:, rank : rank + nstate].reshape(length, seqs, nstate)
    readout = projections[:, rank + nstate :].reshape(length, seqs, nstate)
    return (delta, entry, readout)


def scan_kernel(neg_rate_ref, skip_ref, x_ref, delta_ref, entry_ref, readout_ref, *rest,
                length, reverse, with_init, with_y):
    rest = list(rest)
    init_ref = rest.pop(0) if with_init else None
    y_ref = rest.pop(0) if with_y else None
    state_ref = rest.pop(0)
    nstate = neg_rate_ref.shape[0]
    if with_init:
        state_ref[...] = init_ref[...]
    else:
        state_ref[...] = jnp.zeros(state_ref.shape, state_ref.dtype)

    def step(i, carry):
        t = length - 1 - i if reverse else i
        delta = delta_ref[t]
        x_wide = x_ref[t].astype(jnp.float32)
        drive = delta * x_wide
        entry = entry_ref[t]
        readout = readout_ref[t]
        total = jnp.zeros_like(delta)
        for n in range(nstate):
            state = (
                jnp.exp(delta * neg_rate_ref[pl.ds(n, 1), :]) * state_ref[n]
                + drive * entry[:, n : n + 1]
            )
            state_ref[n] = state
            if with_y:
                total = total + readout[:, n : n + 1] * state
        if with_y:
            y_ref[t] = total + skip_ref[...] * x_wide
        return carry

    lax.fori_loop(0, length, step, 0)


def run_scan(seq_x, delta, entry, readout, neg_rate, skip, init, reverse, with_y):
    length, seqs, inner = delta.shape
    nstate = neg_rate.shape[0]
    state_shape = jax.ShapeDtypeStruct((nstate, seqs, inner), jnp.float32)
    out_shape = [state_shape]
    if with_y:
        out_shape = [jax.ShapeDtypeStruct((length, seqs, inner), jnp.float32), state_shape]
    args = [neg_rate, skip.reshape(1, inner), seq_x, delta, entry, readout]
    if init is not None:
        args.append(init)
    kernel = functools.partial(
        scan_kernel, length=length, reverse=reverse, with_init=init is not None, with_y=with_y
    )
    return pl.pallas_call(kernel, out_shape=tuple(out_shape))(*args)


def combine(earlier, later, neg_rate):
    decay = jnp.exp(later[0][None] * neg_rate[:, None, :])
    return (earlier[0] + later[0], decay * earlier[1] + later[1])


def carried_in(total, end_state, neg_rate, axis, reverse):
    count = lax.axis_size(axis)
    inclusive = (total, end_state)
    exclusive = None
    shift = 1
    while shift < count:
        if reverse:
            pairs = [(i + shift, i) for i in range(count - shift)]
        else:
            pairs = [(i, i + shift) for i in range(count - shift)]
        got = tuple(lax.ppermute(a, axis, pairs) for a in inclusive)
        exclusive = got if exclusive is None else combine(got, exclusive, neg_rate)
        if 2 * shift < count:
            inclusive = combine(got, inclusive, neg_rate)
        shift *= 2
    if exclusive is None:
        return jnp.zeros_like(end_state)
    return exclusive[1]


def direction(seq_x, seq_mask, k, proj_weight, dt_weight, dt_bias, a_rate, skip_d, axis, reverse):
    delta, entry, readout = direction_inputs(
        seq_x, seq_mask, proj_weight[k], dt_weight[k], dt_bias[k]
    )
    neg_rate = -jnp.transpose(a_rate[k])
    (end_state,) = run_scan(seq_x, delta, entry, readout, neg_rate, skip_d[k], None, reverse, False)
    total = jnp.sum(delta, axis=0)
    init = carried_in(total, end_state, neg_rate, axis, reverse)
    y, _ = run_scan(seq_x, delta, entry, readout, neg_rate, skip_d[k], init, reverse, True)
    return y


def local(
    tokens,
    tissue,
    ln_gain,
    in_weight,
    conv_weight,
    conv_bias,
    proj_weight,
    dt_weight,
    dt_bias,
    a_rate,
    skip_d,
    out_gain,
    out_weight,
):
    rows_here, cols_here, width = tokens.shape
    inner = in_weight.shape[1] // 2
    normed = layer_norm(tokens.astype(jnp.float32), ln_gain).astype(jnp.bfloat16)
    projected = jnp.dot(
        normed.reshape(rows_here * cols_here, width), in_weight, preferred_element_type=jnp.float32
    )
    projected = projected.astype(jnp.bfloat16).reshape(rows_here, cols_here, 2 * inner)
    inner_part = projected[:, :, :inner]
    gate_part = projected[:, :, inner:]
    padded = padded_2(inner_part, (("row", 0), ("col", 1)), 1)
    conv_out = conv_silu(padded, conv_weight, conv_bias, rows_here, cols_here)
    tissue_wide = tissue.astype(jnp.float32)
    conv_t = jnp.transpose(conv_out, (1, 0, 2))
    tissue_t = jnp.transpose(tissue_wide)
    common = (proj_weight, dt_weight, dt_bias, a_rate, skip_d)
    along_rows = direction(conv_t, tissue_t, 0, *common, "col", False)
    along_rows = along_rows + direction(conv_t, tissue_t, 2, *common, "col", True)
    along_cols = direction(conv_out, tissue_wide, 1, *common, "row", False)
    along_cols = along_cols + direction(conv_out, tissue_wide, 3, *common, "row", True)
    mixed_sum = jnp.transpose(along_rows, (1, 0, 2)) + along_cols
    mixed = (layer_norm(mixed_sum, out_gain) * jax.nn.silu(gate_part.astype(jnp.float32))).astype(
        jnp.bfloat16
    )
    branch = jnp.dot(
        mixed.reshape(rows_here * cols_here, inner), out_weight, preferred_element_type=jnp.float32
    )
    branch = branch.reshape(rows_here, cols_here, width)
    return (tokens.astype(jnp.float32) + tissue_wide[:, :, None] * branch).astype(jnp.bfloat16)


def solution(mesh):
    return jax.shard_map(
        local,
        mesh=mesh,
        in_specs=(
            P("row", "col", None),
            P("row", "col"),
            P(),
            P(),
            P(),
            P(),
            P(),
            P(),
            P(),
            P(),
            P(),
            P(),
            P(),
        ),
        out_specs=P("row", "col", None),
        check_vma=False,
    )
```

```python
import functools

import jax
import jax.numpy as jnp
from jax import lax
from jax.experimental import pallas as pl
from jax.sharding import PartitionSpec as P


def padded_2(block, sides, width):
    for axis, dim in sides:
        count = axis_count(axis)
        forward = [(i, i + 1) for i in range(count - 1)]
        backward = [(target, source) for source, target in forward]
        low = lax.ppermute(
            lax.slice_in_dim(block, block.shape[dim] - width, None, axis=dim), axis, forward
        )
        high = lax.ppermute(lax.slice_in_dim(block, 0, width, axis=dim), axis, backward)
        block = jnp.concatenate([low, block, high], axis=dim)
    return block


def axis_count(axis):
    if isinstance(axis, tuple):
        count = 1
        for name in axis:
            count *= lax.axis_size(name)
        return count
    return lax.axis_size(axis)


def layer_norm(values, gain):
    center = values - jnp.mean(values, axis=-1, keepdims=True)
    spread = jnp.mean(center * center, axis=-1, keepdims=True)
    return center * lax.rsqrt(spread + 1e-05) * gain


def conv_silu(padded, conv_weight, conv_bias, height, width):
    summed = jnp.broadcast_to(conv_bias, (height, width, conv_bias.shape[0]))
    for offset_row in range(3):
        for offset_col in range(3):
            window = padded[offset_row : offset_row + height, offset_col : offset_col + width]
            summed = summed + window.astype(jnp.float32) * conv_weight[
                offset_row, offset_col
            ].astype(jnp.float32)
    return jax.nn.silu(summed).astype(jnp.bfloat16)


def direction_inputs(seq_x, seq_mask, proj_one, dtw_one, dtb_one):
    rank = dtw_one.shape[0]
    nstate = (proj_one.shape[1] - rank) // 2
    length, seqs, inner = seq_x.shape
    flat = seq_x.reshape(length * seqs, inner)
    projections = jnp.dot(flat, proj_one, preferred_element_type=jnp.float32)
    rate_low = projections[:, :rank].astype(jnp.bfloat16)
    delta = jax.nn.softplus(
        jnp.dot(rate_low, dtw_one, preferred_element_type=jnp.float32) + dtb_one
    )
    delta = delta.reshape(length, seqs, inner) * seq_mask[:, :, None]
    entry = projections[:, rank : rank + nstate].reshape(length, seqs, nstate)
    readout = projections[:, rank + nstate :].reshape(length, seqs, nstate)
    return (delta, entry, readout)


def scan_kernel(neg_rate_ref, skip_ref, x_ref, delta_ref, entry_ref, readout_ref, *rest,
                length, reverse, with_init, with_y):
    rest = list(rest)
    init_ref = rest.pop(0) if with_init else None
    y_ref = rest.pop(0) if with_y else None
    state_ref = rest.pop(0)
    nstate = neg_rate_ref.shape[0]
    if with_init:
        state_ref[...] = init_ref[...]
    else:
        state_ref[...] = jnp.zeros(state_ref.shape, state_ref.dtype)

    def step(i, summed):
        t = length - 1 - i if reverse else i
        delta = delta_ref[t]
        x_wide = x_ref[t].astype(jnp.float32)
        drive = delta * x_wide
        entry = entry_ref[t]
        readout = readout_ref[t]
        total = jnp.zeros_like(delta)
        for n in range(nstate):
            state = (
                jnp.exp(delta * neg_rate_ref[pl.ds(n, 1), :]) * state_ref[n]
                + drive * entry[:, n : n + 1]
            )
            state_ref[n] = state
            if with_y:
                total = total + readout[:, n : n + 1] * state
        if with_y:
            y_ref[t] = total + skip_ref[...] * x_wide
        return summed + delta

    summed = lax.fori_loop(0, length, step, jnp.zeros(state_ref.shape[1:], jnp.float32))
    state_ref[nstate] = summed


def run_scan(seq_x, delta, entry, readout, neg_rate, skip, init, reverse, with_y):
    length, seqs, inner = delta.shape
    nstate = neg_rate.shape[0]
    state_shape = jax.ShapeDtypeStruct((nstate + 1, seqs, inner), jnp.float32)
    out_shape = [state_shape]
    if with_y:
        out_shape = [jax.ShapeDtypeStruct((length, seqs, inner), jnp.float32), state_shape]
    args = [neg_rate, skip.reshape(1, inner), seq_x, delta, entry, readout]
    if init is not None:
        args.append(init)
    kernel = functools.partial(
        scan_kernel, length=length, reverse=reverse, with_init=init is not None, with_y=with_y
    )
    return pl.pallas_call(kernel, out_shape=tuple(out_shape))(*args)


def combine(earlier, later, neg_rate):
    nstate = neg_rate.shape[0]
    decay = jnp.exp(later[nstate][None] * neg_rate[:, None, :])
    state = decay * earlier[:nstate] + later[:nstate]
    return jnp.concatenate([state, (earlier[nstate] + later[nstate])[None]], axis=0)


def carried_in(packed, neg_rate, axis, reverse):
    count = lax.axis_size(axis)
    inclusive = packed
    exclusive = None
    shift = 1
    while shift < count:
        if reverse:
            pairs = [(i + shift, i) for i in range(count - shift)]
        else:
            pairs = [(i, i + shift) for i in range(count - shift)]
        got = lax.ppermute(inclusive, axis, pairs)
        exclusive = got if exclusive is None else combine(got, exclusive, neg_rate)
        if 2 * shift < count:
            inclusive = combine(got, inclusive, neg_rate)
        shift *= 2
    if exclusive is None:
        return jnp.zeros_like(packed)
    return exclusive


def direction(seq_x, seq_mask, k, proj_weight, dt_weight, dt_bias, a_rate, skip_d, axis, reverse):
    delta, entry, readout = direction_inputs(
        seq_x, seq_mask, proj_weight[k], dt_weight[k], dt_bias[k]
    )
    neg_rate = -jnp.transpose(a_rate[k])
    (packed,) = run_scan(seq_x, delta, entry, readout, neg_rate, skip_d[k], None, reverse, False)
    init = carried_in(packed, neg_rate, axis, reverse)
    y, _ = run_scan(seq_x, delta, entry, readout, neg_rate, skip_d[k], init, reverse, True)
    return y


def local(
    tokens,
    tissue,
    ln_gain,
    in_weight,
    conv_weight,
    conv_bias,
    proj_weight,
    dt_weight,
    dt_bias,
    a_rate,
    skip_d,
    out_gain,
    out_weight,
):
    rows_here, cols_here, width = tokens.shape
    inner = in_weight.shape[1] // 2
    normed = layer_norm(tokens.astype(jnp.float32), ln_gain).astype(jnp.bfloat16)
    projected = jnp.dot(
        normed.reshape(rows_here * cols_here, width), in_weight, preferred_element_type=jnp.float32
    )
    projected = projected.astype(jnp.bfloat16).reshape(rows_here, cols_here, 2 * inner)
    inner_part = projected[:, :, :inner]
    gate_part = projected[:, :, inner:]
    padded = padded_2(inner_part, (("row", 0), (("cx", "cz"), 1)), 1)
    conv_out = conv_silu(padded, conv_weight, conv_bias, rows_here, cols_here)
    tissue_wide = tissue.astype(jnp.float32)
    band_x = lax.all_to_all(conv_out, "cz", 0, 1, tiled=True)
    band_mask = lax.all_to_all(tissue_wide, "cz", 0, 1, tiled=True)
    conv_t = jnp.transpose(band_x, (1, 0, 2))
    tissue_t = jnp.transpose(band_mask)
    common = (proj_weight, dt_weight, dt_bias, a_rate, skip_d)
    along_rows = direction(conv_t, tissue_t, 0, *common, "cx", False)
    along_rows = along_rows + direction(conv_t, tissue_t, 2, *common, "cx", True)
    along_rows = lax.all_to_all(along_rows, "cz", 0, 1, tiled=True)
    along_cols = direction(conv_out, tissue_wide, 1, *common, "row", False)
    along_cols = along_cols + direction(conv_out, tissue_wide, 3, *common, "row", True)
    mixed_sum = jnp.transpose(along_rows, (1, 0, 2)) + along_cols
    mixed = (layer_norm(mixed_sum, out_gain) * jax.nn.silu(gate_part.astype(jnp.float32))).astype(
        jnp.bfloat16
    )
    branch = jnp.dot(
        mixed.reshape(rows_here * cols_here, inner), out_weight, preferred_element_type=jnp.float32
    )
    branch = branch.reshape(rows_here, cols_here, width)
    return (tokens.astype(jnp.float32) + tissue_wide[:, :, None] * branch).astype(jnp.bfloat16)


def solution(mesh):
    cols = mesh.shape["col"]
    group = 8 if cols % 8 == 0 else cols
    grid = mesh.devices.reshape(mesh.shape["row"], cols // group, group)
    mesh = jax.sharding.Mesh(grid, ("row", "cx", "cz"))
    col = ("cx", "cz")
    return jax.shard_map(
        local,
        mesh=mesh,
        in_specs=(
            P("row", col, None),
            P("row", col),
            P(),
            P(),
            P(),
            P(),
            P(),
            P(),
            P(),
            P(),
            P(),
            P(),
            P(),
        ),
        out_specs=P("row", col, None),
        check_vma=False,
    )
```

```python
import functools

import jax
import jax.numpy as jnp
from jax import lax
from jax.experimental import pallas as pl
from jax.sharding import PartitionSpec as P


def padded_2(block, sides, width):
    for axis, dim in sides:
        count = axis_count(axis)
        forward = [(i, i + 1) for i in range(count - 1)]
        backward = [(target, source) for source, target in forward]
        low = lax.ppermute(
            lax.slice_in_dim(block, block.shape[dim] - width, None, axis=dim), axis, forward
        )
        high = lax.ppermute(lax.slice_in_dim(block, 0, width, axis=dim), axis, backward)
        block = jnp.concatenate([low, block, high], axis=dim)
    return block


def axis_count(axis):
    if isinstance(axis, tuple):
        count = 1
        for name in axis:
            count *= lax.axis_size(name)
        return count
    return lax.axis_size(axis)


def layer_norm(values, gain):
    center = values - jnp.mean(values, axis=-1, keepdims=True)
    spread = jnp.mean(center * center, axis=-1, keepdims=True)
    return center * lax.rsqrt(spread + 1e-05) * gain


def conv_silu(padded, conv_weight, conv_bias, height, width):
    summed = jnp.broadcast_to(conv_bias, (height, width, conv_bias.shape[0]))
    for offset_row in range(3):
        for offset_col in range(3):
            window = padded[offset_row : offset_row + height, offset_col : offset_col + width]
            summed = summed + window.astype(jnp.float32) * conv_weight[
                offset_row, offset_col
            ].astype(jnp.float32)
    return jax.nn.silu(summed).astype(jnp.bfloat16)


def direction_inputs(seq_x, seq_mask, proj_one, dtw_one, dtb_one):
    rank = dtw_one.shape[0]
    nstate = (proj_one.shape[1] - rank) // 2
    length, seqs, inner = seq_x.shape
    flat = seq_x.reshape(length * seqs, inner)
    projections = jnp.dot(flat, proj_one, preferred_element_type=jnp.float32)
    rate_low = projections[:, :rank].astype(jnp.bfloat16)
    delta = jax.nn.softplus(
        jnp.dot(rate_low, dtw_one, preferred_element_type=jnp.float32) + dtb_one
    )
    delta = delta.reshape(length, seqs, inner) * seq_mask[:, :, None]
    entry = projections[:, rank : rank + nstate].reshape(length, seqs, nstate)
    readout = projections[:, rank + nstate :].reshape(length, seqs, nstate)
    return (delta, entry, readout)


def scan_kernel(neg_rate_ref, skip_ref, x_ref, delta_ref, entry_ref, readout_ref, *rest,
                length, reverse, with_init, with_y):
    rest = list(rest)
    init_ref = rest.pop(0) if with_init else None
    y_ref = rest.pop(0) if with_y else None
    state_ref = rest.pop(0)
    nstate = neg_rate_ref.shape[0]
    if with_init:
        state_ref[...] = init_ref[...]
    else:
        state_ref[...] = jnp.zeros(state_ref.shape, state_ref.dtype)

    def step(i, summed):
        t = length - 1 - i if reverse else i
        delta = delta_ref[t]
        x_wide = x_ref[t].astype(jnp.float32)
        drive = delta * x_wide
        entry = entry_ref[t]
        readout = readout_ref[t]
        total = jnp.zeros_like(delta)
        for n in range(nstate):
            state = (
                jnp.exp(delta * neg_rate_ref[n]) * state_ref[n]
                + drive * entry[:, n : n + 1]
            )
            state_ref[n] = state
            if with_y:
                total = total + readout[:, n : n + 1] * state
        if with_y:
            y_ref[t] = total + skip_ref[...] * x_wide
        return summed + delta

    summed = lax.fori_loop(0, length, step, jnp.zeros(state_ref.shape[1:], jnp.float32))
    state_ref[nstate] = summed


def run_scan(seq_x, delta, entry, readout, neg_rate, skip, init, reverse, with_y):
    length, seqs, inner = delta.shape
    nstate = neg_rate.shape[0]
    state_shape = jax.ShapeDtypeStruct((nstate + 1, seqs, inner), jnp.float32)
    out_shape = [state_shape]
    if with_y:
        out_shape = [jax.ShapeDtypeStruct((length, seqs, inner), jnp.float32), state_shape]
    args = [neg_rate, skip, seq_x, delta, entry, readout]
    if init is not None:
        args.append(init)
    kernel = functools.partial(
        scan_kernel, length=length, reverse=reverse, with_init=init is not None, with_y=with_y
    )
    return pl.pallas_call(kernel, out_shape=tuple(out_shape))(*args)


def combine(earlier, later, neg_rate):
    nstate = neg_rate.shape[0]
    decay = jnp.exp(later[nstate][None] * neg_rate[:, None, :])
    state = decay * earlier[:nstate] + later[:nstate]
    return jnp.concatenate([state, (earlier[nstate] + later[nstate])[None]], axis=0)


def carried_in(packed, neg_rate, axis, reverse):
    count = lax.axis_size(axis)
    inclusive = packed
    exclusive = None
    shift = 1
    while shift < count:
        if reverse:
            pairs = [(i + shift, i) for i in range(count - shift)]
        else:
            pairs = [(i, i + shift) for i in range(count - shift)]
        got = lax.ppermute(inclusive, axis, pairs)
        exclusive = got if exclusive is None else combine(got, exclusive, neg_rate)
        if 2 * shift < count:
            inclusive = combine(got, inclusive, neg_rate)
        shift *= 2
    if exclusive is None:
        return jnp.zeros_like(packed)
    return exclusive


def flipped(array):
    return array[::-1]


def rows_of(value, seqs):
    return jnp.broadcast_to(value[..., None, :], value.shape[:-1] + (seqs, value.shape[-1]))


def direction_pair(seq_x, seq_mask, ahead, back, proj_weight, dt_weight, dt_bias, a_rate, skip_d,
                   axis):
    length, seqs, inner = seq_x.shape
    nstate = a_rate.shape[2]
    fwd = direction_inputs(seq_x, seq_mask, proj_weight[ahead], dt_weight[ahead], dt_bias[ahead])
    bwd = direction_inputs(seq_x, seq_mask, proj_weight[back], dt_weight[back], dt_bias[back])
    both = [jnp.concatenate([f, flipped(b)], axis=1) for f, b in zip(fwd, bwd)]
    delta, entry, readout = both
    stacked_x = jnp.concatenate([seq_x, flipped(seq_x)], axis=1)
    neg_fwd = -jnp.transpose(a_rate[ahead])
    neg_bwd = -jnp.transpose(a_rate[back])
    neg_rate = jnp.concatenate([rows_of(neg_fwd, seqs), rows_of(neg_bwd, seqs)], axis=1)
    skip = jnp.concatenate([rows_of(skip_d[ahead], seqs), rows_of(skip_d[back], seqs)], axis=0)
    (packed,) = run_scan(stacked_x, delta, entry, readout, neg_rate, skip, None, False, False)
    init_fwd = carried_in(packed[:, :seqs], neg_fwd, axis, False)
    init_bwd = carried_in(packed[:, seqs:], neg_bwd, axis, True)
    init = jnp.concatenate([init_fwd, init_bwd], axis=1)
    y, _ = run_scan(stacked_x, delta, entry, readout, neg_rate, skip, init, False, True)
    return y[:, :seqs] + flipped(y[:, seqs:])


def local(
    tokens,
    tissue,
    ln_gain,
    in_weight,
    conv_weight,
    conv_bias,
    proj_weight,
    dt_weight,
    dt_bias,
    a_rate,
    skip_d,
    out_gain,
    out_weight,
):
    rows_here, cols_here, width = tokens.shape
    inner = in_weight.shape[1] // 2
    normed = layer_norm(tokens.astype(jnp.float32), ln_gain).astype(jnp.bfloat16)
    projected = jnp.dot(
        normed.reshape(rows_here * cols_here, width), in_weight, preferred_element_type=jnp.float32
    )
    projected = projected.astype(jnp.bfloat16).reshape(rows_here, cols_here, 2 * inner)
    inner_part = projected[:, :, :inner]
    gate_part = projected[:, :, inner:]
    padded = padded_2(inner_part, (("row", 0), (("cx", "cz"), 1)), 1)
    conv_out = conv_silu(padded, conv_weight, conv_bias, rows_here, cols_here)
    tissue_wide = tissue.astype(jnp.float32)
    group = lax.axis_size("cz")
    mask_lane = jnp.pad(tissue.astype(jnp.bfloat16), ((0, 0), (0, inner - cols_here)))
    sent = jnp.concatenate([conv_out, mask_lane[:, None, :]], axis=1)
    band = lax.all_to_all(sent, "cz", 0, 1, tiled=True)
    band = band.reshape(rows_here // group, group, cols_here + 1, inner)
    band_x = band[:, :, :cols_here, :].reshape(rows_here // group, group * cols_here, inner)
    band_mask = band[:, :, cols_here, :cols_here].reshape(rows_here // group, group * cols_here)
    conv_t = jnp.transpose(band_x, (1, 0, 2))
    tissue_t = jnp.transpose(band_mask).astype(jnp.float32)
    common = (proj_weight, dt_weight, dt_bias, a_rate, skip_d)
    along_rows = direction_pair(conv_t, tissue_t, 0, 2, *common, "cx")
    along_rows = lax.all_to_all(along_rows, "cz", 0, 1, tiled=True)
    along_cols = direction_pair(conv_out, tissue_wide, 1, 3, *common, "row")
    mixed_sum = jnp.transpose(along_rows, (1, 0, 2)) + along_cols
    mixed = (layer_norm(mixed_sum, out_gain) * jax.nn.silu(gate_part.astype(jnp.float32))).astype(
        jnp.bfloat16
    )
    branch = jnp.dot(
        mixed.reshape(rows_here * cols_here, inner), out_weight, preferred_element_type=jnp.float32
    )
    branch = branch.reshape(rows_here, cols_here, width)
    return (tokens.astype(jnp.float32) + tissue_wide[:, :, None] * branch).astype(jnp.bfloat16)


def solution(mesh):
    cols = mesh.shape["col"]
    group = 8 if cols % 8 == 0 else cols
    grid = mesh.devices.reshape(mesh.shape["row"], cols // group, group)
    mesh = jax.sharding.Mesh(grid, ("row", "cx", "cz"))
    col = ("cx", "cz")
    return jax.shard_map(
        local,
        mesh=mesh,
        in_specs=(
            P("row", col, None),
            P("row", col),
            P(),
            P(),
            P(),
            P(),
            P(),
            P(),
            P(),
            P(),
            P(),
            P(),
            P(),
        ),
        out_specs=P("row", col, None),
        check_vma=False,
    )
```

```python
import functools

import jax
import jax.numpy as jnp
from jax import lax
from jax.experimental import pallas as pl
from jax.sharding import PartitionSpec as P


def padded_2(block, sides, width):
    for axis, dim in sides:
        count = axis_count(axis)
        forward = [(i, i + 1) for i in range(count - 1)]
        backward = [(target, source) for source, target in forward]
        low = lax.ppermute(
            lax.slice_in_dim(block, block.shape[dim] - width, None, axis=dim), axis, forward
        )
        high = lax.ppermute(lax.slice_in_dim(block, 0, width, axis=dim), axis, backward)
        block = jnp.concatenate([low, block, high], axis=dim)
    return block


def axis_count(axis):
    if isinstance(axis, tuple):
        count = 1
        for name in axis:
            count *= lax.axis_size(name)
        return count
    return lax.axis_size(axis)


def layer_norm(values, gain):
    center = values - jnp.mean(values, axis=-1, keepdims=True)
    spread = jnp.mean(center * center, axis=-1, keepdims=True)
    return center * lax.rsqrt(spread + 1e-05) * gain


def conv_silu(padded, conv_weight, conv_bias, height, width):
    summed = jnp.broadcast_to(conv_bias, (height, width, conv_bias.shape[0]))
    for offset_row in range(3):
        for offset_col in range(3):
            window = padded[offset_row : offset_row + height, offset_col : offset_col + width]
            summed = summed + window.astype(jnp.float32) * conv_weight[
                offset_row, offset_col
            ].astype(jnp.float32)
    return jax.nn.silu(summed).astype(jnp.bfloat16)


def direction_inputs(seq_x, seq_mask, proj_one, dtw_one, dtb_one):
    rank = dtw_one.shape[0]
    nstate = (proj_one.shape[1] - rank) // 2
    length, seqs, inner = seq_x.shape
    flat = seq_x.reshape(length * seqs, inner)
    projections = jnp.dot(flat, proj_one, preferred_element_type=jnp.float32)
    rate_low = projections[:, :rank].astype(jnp.bfloat16)
    delta = jax.nn.softplus(
        jnp.dot(rate_low, dtw_one, preferred_element_type=jnp.float32) + dtb_one
    )
    delta = delta.reshape(length, seqs, inner) * seq_mask[:, :, None]
    entry = projections[:, rank : rank + nstate].reshape(length, seqs, nstate)
    readout = projections[:, rank + nstate :].reshape(length, seqs, nstate)
    return (delta, entry, readout)


def scan_kernel(neg_rate_ref, skip_ref, x_ref, delta_ref, entry_ref, readout_ref, *rest,
                length, reverse, with_init, with_y):
    rest = list(rest)
    init_ref = rest.pop(0) if with_init else None
    y_ref = rest.pop(0) if with_y else None
    state_ref = rest.pop(0)
    nstate = neg_rate_ref.shape[0]
    if with_init:
        state_ref[...] = init_ref[...]
    else:
        state_ref[...] = jnp.zeros(state_ref.shape, state_ref.dtype)

    def step(i, summed):
        t = length - 1 - i if reverse else i
        delta = delta_ref[t]
        x_wide = x_ref[t].astype(jnp.float32)
        drive = delta * x_wide
        entry = entry_ref[t]
        readout = readout_ref[t]
        total = jnp.zeros_like(delta)
        for n in range(nstate):
            state = (
                jnp.exp(delta * neg_rate_ref[n]) * state_ref[n]
                + drive * entry[:, n : n + 1]
            )
            state_ref[n] = state
            if with_y:
                total = total + readout[:, n : n + 1] * state
        if with_y:
            y_ref[t] = total + skip_ref[...] * x_wide
        return summed + delta

    summed = lax.fori_loop(0, length, step, jnp.zeros(state_ref.shape[1:], jnp.float32))
    state_ref[nstate] = summed


def run_scan(seq_x, delta, entry, readout, neg_rate, skip, init, reverse, with_y):
    length, seqs, inner = delta.shape
    nstate = neg_rate.shape[0]
    state_shape = jax.ShapeDtypeStruct((nstate + 1, seqs, inner), jnp.float32)
    out_shape = [state_shape]
    if with_y:
        out_shape = [jax.ShapeDtypeStruct((length, seqs, inner), jnp.float32), state_shape]
    args = [neg_rate, skip, seq_x, delta, entry, readout]
    if init is not None:
        args.append(init)
    kernel = functools.partial(
        scan_kernel, length=length, reverse=reverse, with_init=init is not None, with_y=with_y
    )
    return pl.pallas_call(kernel, out_shape=tuple(out_shape))(*args)


def combine(earlier, later, neg_rate):
    nstate = neg_rate.shape[0]
    decay = jnp.exp(later[nstate][None] * neg_rate[:, None, :])
    state = decay * earlier[:nstate] + later[:nstate]
    return jnp.concatenate([state, (earlier[nstate] + later[nstate])[None]], axis=0)


def carried_in(packed, neg_rate, axis, reverse):
    count = lax.axis_size(axis)
    inclusive = packed
    exclusive = None
    shift = 1
    while shift < count:
        if reverse:
            pairs = [(i + shift, i) for i in range(count - shift)]
        else:
            pairs = [(i, i + shift) for i in range(count - shift)]
        got = lax.ppermute(inclusive, axis, pairs)
        exclusive = got if exclusive is None else combine(got, exclusive, neg_rate)
        if 2 * shift < count:
            inclusive = combine(got, inclusive, neg_rate)
        shift *= 2
    if exclusive is None:
        return jnp.zeros_like(packed)
    return exclusive


def flipped(array):
    return array[::-1]


def rows_of(value, seqs):
    return jnp.broadcast_to(value[..., None, :], value.shape[:-1] + (seqs, value.shape[-1]))


def pair_inputs(stacked_x, stacked_mask, ahead, back, proj_weight, dt_weight, dt_bias, seqs):
    rank = dt_weight.shape[1]
    length, both_seqs, inner = stacked_x.shape
    flat = stacked_x.reshape(length * both_seqs, inner)
    weights = jnp.concatenate([proj_weight[ahead], proj_weight[back]], axis=1)
    width = proj_weight.shape[2]
    projections = jnp.dot(flat, weights, preferred_element_type=jnp.float32)
    projections = projections.reshape(length, both_seqs, 2 * width)
    is_fwd = (lax.broadcasted_iota(jnp.int32, (1, both_seqs, 1), 1) < seqs)
    chosen = jnp.where(is_fwd, projections[:, :, :width], projections[:, :, width:])
    rate_low = chosen[:, :, :rank].astype(jnp.bfloat16).reshape(length * both_seqs, rank)
    step_fwd = jnp.dot(rate_low, dt_weight[ahead], preferred_element_type=jnp.float32)
    step_bwd = jnp.dot(rate_low, dt_weight[back], preferred_element_type=jnp.float32)
    step_fwd = step_fwd.reshape(length, both_seqs, inner) + dt_bias[ahead]
    step_bwd = step_bwd.reshape(length, both_seqs, inner) + dt_bias[back]
    delta = jax.nn.softplus(jnp.where(is_fwd, step_fwd, step_bwd)) * stacked_mask[:, :, None]
    nstate = (width - rank) // 2
    entry = chosen[:, :, rank : rank + nstate]
    readout = chosen[:, :, rank + nstate :]
    return (delta, entry, readout)


def direction_pair(seq_x, seq_mask, ahead, back, proj_weight, dt_weight, dt_bias, a_rate, skip_d,
                   axis):
    length, seqs, inner = seq_x.shape
    stacked_x = jnp.concatenate([seq_x, flipped(seq_x)], axis=1)
    stacked_mask = jnp.concatenate([seq_mask, flipped(seq_mask)], axis=1)
    delta, entry, readout = pair_inputs(
        stacked_x, stacked_mask, ahead, back, proj_weight, dt_weight, dt_bias, seqs
    )
    neg_fwd = -jnp.transpose(a_rate[ahead])
    neg_bwd = -jnp.transpose(a_rate[back])
    neg_rate = jnp.concatenate([rows_of(neg_fwd, seqs), rows_of(neg_bwd, seqs)], axis=1)
    skip = jnp.concatenate([rows_of(skip_d[ahead], seqs), rows_of(skip_d[back], seqs)], axis=0)
    (packed,) = run_scan(stacked_x, delta, entry, readout, neg_rate, skip, None, False, False)
    init_fwd = carried_in(packed[:, :seqs], neg_fwd, axis, False)
    init_bwd = carried_in(packed[:, seqs:], neg_bwd, axis, True)
    init = jnp.concatenate([init_fwd, init_bwd], axis=1)
    y, _ = run_scan(stacked_x, delta, entry, readout, neg_rate, skip, init, False, True)
    return y[:, :seqs] + flipped(y[:, seqs:])


def local(
    tokens,
    tissue,
    ln_gain,
    in_weight,
    conv_weight,
    conv_bias,
    proj_weight,
    dt_weight,
    dt_bias,
    a_rate,
    skip_d,
    out_gain,
    out_weight,
):
    rows_here, cols_here, width = tokens.shape
    inner = in_weight.shape[1] // 2
    normed = layer_norm(tokens.astype(jnp.float32), ln_gain).astype(jnp.bfloat16)
    projected = jnp.dot(
        normed.reshape(rows_here * cols_here, width), in_weight, preferred_element_type=jnp.float32
    )
    projected = projected.astype(jnp.bfloat16).reshape(rows_here, cols_here, 2 * inner)
    inner_part = projected[:, :, :inner]
    gate_part = projected[:, :, inner:]
    padded = padded_2(inner_part, (("row", 0), (("cx", "cz"), 1)), 1)
    conv_out = conv_silu(padded, conv_weight, conv_bias, rows_here, cols_here)
    tissue_wide = tissue.astype(jnp.float32)
    group = lax.axis_size("cz")
    mask_lane = jnp.pad(tissue.astype(jnp.bfloat16), ((0, 0), (0, inner - cols_here)))
    sent = jnp.concatenate([conv_out, mask_lane[:, None, :]], axis=1)
    band = lax.all_to_all(sent, "cz", 0, 1, tiled=True)
    band = band.reshape(rows_here // group, group, cols_here + 1, inner)
    band_x = band[:, :, :cols_here, :].reshape(rows_here // group, group * cols_here, inner)
    band_mask = band[:, :, cols_here, :cols_here].reshape(rows_here // group, group * cols_here)
    conv_t = jnp.transpose(band_x, (1, 0, 2))
    tissue_t = jnp.transpose(band_mask).astype(jnp.float32)
    common = (proj_weight, dt_weight, dt_bias, a_rate, skip_d)
    along_rows = direction_pair(conv_t, tissue_t, 0, 2, *common, "cx")
    along_rows = lax.all_to_all(along_rows, "cz", 0, 1, tiled=True)
    along_cols = direction_pair(conv_out, tissue_wide, 1, 3, *common, "row")
    mixed_sum = jnp.transpose(along_rows, (1, 0, 2)) + along_cols
    mixed = (layer_norm(mixed_sum, out_gain) * jax.nn.silu(gate_part.astype(jnp.float32))).astype(
        jnp.bfloat16
    )
    branch = jnp.dot(
        mixed.reshape(rows_here * cols_here, inner), out_weight, preferred_element_type=jnp.float32
    )
    branch = branch.reshape(rows_here, cols_here, width)
    return (tokens.astype(jnp.float32) + tissue_wide[:, :, None] * branch).astype(jnp.bfloat16)


def solution(mesh):
    cols = mesh.shape["col"]
    group = 8 if cols % 8 == 0 else cols
    grid = mesh.devices.reshape(mesh.shape["row"], cols // group, group)
    mesh = jax.sharding.Mesh(grid, ("row", "cx", "cz"))
    col = ("cx", "cz")
    return jax.shard_map(
        local,
        mesh=mesh,
        in_specs=(
            P("row", col, None),
            P("row", col),
            P(),
            P(),
            P(),
            P(),
            P(),
            P(),
            P(),
            P(),
            P(),
            P(),
            P(),
        ),
        out_specs=P("row", col, None),
        check_vma=False,
    )
```

```python
import functools

import jax
import jax.numpy as jnp
from jax import lax
from jax.experimental import pallas as pl
from jax.sharding import PartitionSpec as P


def padded_2(block, sides, width):
    for axis, dim in sides:
        count = axis_count(axis)
        forward = [(i, i + 1) for i in range(count - 1)]
        backward = [(target, source) for source, target in forward]
        low = lax.ppermute(
            lax.slice_in_dim(block, block.shape[dim] - width, None, axis=dim), axis, forward
        )
        high = lax.ppermute(lax.slice_in_dim(block, 0, width, axis=dim), axis, backward)
        block = jnp.concatenate([low, block, high], axis=dim)
    return block


def axis_count(axis):
    if isinstance(axis, tuple):
        count = 1
        for name in axis:
            count *= lax.axis_size(name)
        return count
    return lax.axis_size(axis)


def layer_norm(values, gain):
    center = values - jnp.mean(values, axis=-1, keepdims=True)
    spread = jnp.mean(center * center, axis=-1, keepdims=True)
    return center * lax.rsqrt(spread + 1e-05) * gain


def conv_silu(padded, conv_weight, conv_bias, height, width):
    summed = jnp.broadcast_to(conv_bias, (height, width, conv_bias.shape[0]))
    for offset_row in range(3):
        for offset_col in range(3):
            window = padded[offset_row : offset_row + height, offset_col : offset_col + width]
            summed = summed + window.astype(jnp.float32) * conv_weight[
                offset_row, offset_col
            ].astype(jnp.float32)
    return jax.nn.silu(summed).astype(jnp.bfloat16)


def direction_inputs(seq_x, seq_mask, proj_one, dtw_one, dtb_one):
    rank = dtw_one.shape[0]
    nstate = (proj_one.shape[1] - rank) // 2
    length, seqs, inner = seq_x.shape
    flat = seq_x.reshape(length * seqs, inner)
    projections = jnp.dot(flat, proj_one, preferred_element_type=jnp.float32)
    rate_low = projections[:, :rank].astype(jnp.bfloat16)
    delta = jax.nn.softplus(
        jnp.dot(rate_low, dtw_one, preferred_element_type=jnp.float32) + dtb_one
    )
    delta = delta.reshape(length, seqs, inner) * seq_mask[:, :, None]
    entry = projections[:, rank : rank + nstate].reshape(length, seqs, nstate)
    readout = projections[:, rank + nstate :].reshape(length, seqs, nstate)
    return (delta, entry, readout)


def scan_kernel(neg_rate_ref, skip_ref, x_ref, delta_ref, entry_ref, readout_ref, *rest,
                length, reverse, with_init, with_y):
    rest = list(rest)
    init_ref = rest.pop(0) if with_init else None
    y_ref = rest.pop(0) if with_y else None
    state_ref = rest.pop(0)
    nstate = neg_rate_ref.shape[0]
    slab = state_ref.shape[1:]
    in_registers = slab[0] <= 8
    if in_registers:
        if with_init:
            start = tuple(init_ref[n] for n in range(nstate))
        else:
            start = tuple(jnp.zeros(slab, jnp.float32) for _ in range(nstate))
    else:
        start = ()
        if with_init:
            state_ref[...] = init_ref[...]
        else:
            state_ref[...] = jnp.zeros(state_ref.shape, state_ref.dtype)

    def step(i, carry):
        summed, states = carry
        t = length - 1 - i if reverse else i
        delta = delta_ref[t]
        x_wide = x_ref[t].astype(jnp.float32)
        drive = delta * x_wide
        entry = entry_ref[t]
        readout = readout_ref[t]
        total = jnp.zeros_like(delta)
        kept = []
        for n in range(nstate):
            before = states[n] if in_registers else state_ref[n]
            state = jnp.exp(delta * neg_rate_ref[n]) * before + drive * entry[:, n : n + 1]
            if in_registers:
                kept.append(state)
            else:
                state_ref[n] = state
            if with_y:
                total = total + readout[:, n : n + 1] * state
        if with_y:
            y_ref[t] = total + skip_ref[...] * x_wide
        return (summed + delta, tuple(kept))

    summed, states = lax.fori_loop(
        0, length, step, (jnp.zeros(slab, jnp.float32), start), unroll=4 if in_registers else 2
    )
    for n, state in enumerate(states):
        state_ref[n] = state
    state_ref[nstate] = summed


def run_scan(seq_x, delta, entry, readout, neg_rate, skip, init, reverse, with_y):
    length, seqs, inner = delta.shape
    nstate = neg_rate.shape[0]
    state_shape = jax.ShapeDtypeStruct((nstate + 1, seqs, inner), jnp.float32)
    out_shape = [state_shape]
    if with_y:
        out_shape = [jax.ShapeDtypeStruct((length, seqs, inner), jnp.float32), state_shape]
    args = [neg_rate, skip, seq_x, delta, entry, readout]
    if init is not None:
        args.append(init)
    kernel = functools.partial(
        scan_kernel, length=length, reverse=reverse, with_init=init is not None, with_y=with_y
    )
    return pl.pallas_call(kernel, out_shape=tuple(out_shape))(*args)


def combine(earlier, later, neg_rate):
    nstate = neg_rate.shape[0]
    decay = jnp.exp(later[nstate][None] * neg_rate[:, None, :])
    state = decay * earlier[:nstate] + later[:nstate]
    return jnp.concatenate([state, (earlier[nstate] + later[nstate])[None]], axis=0)


def carried_in(packed, neg_rate, axis, reverse):
    count = lax.axis_size(axis)
    inclusive = packed
    exclusive = None
    shift = 1
    while shift < count:
        if reverse:
            pairs = [(i + shift, i) for i in range(count - shift)]
        else:
            pairs = [(i, i + shift) for i in range(count - shift)]
        got = lax.ppermute(inclusive, axis, pairs)
        exclusive = got if exclusive is None else combine(got, exclusive, neg_rate)
        if 2 * shift < count:
            inclusive = combine(got, inclusive, neg_rate)
        shift *= 2
    if exclusive is None:
        return jnp.zeros_like(packed)
    return exclusive


def flipped(array):
    return array[::-1]


def rows_of(value, seqs):
    return jnp.broadcast_to(value[..., None, :], value.shape[:-1] + (seqs, value.shape[-1]))


def pair_inputs(stacked_x, stacked_mask, ahead, back, proj_weight, dt_weight, dt_bias, seqs):
    rank = dt_weight.shape[1]
    length, both_seqs, inner = stacked_x.shape
    flat = stacked_x.reshape(length * both_seqs, inner)
    weights = jnp.concatenate([proj_weight[ahead], proj_weight[back]], axis=1)
    width = proj_weight.shape[2]
    projections = jnp.dot(flat, weights, preferred_element_type=jnp.float32)
    projections = projections.reshape(length, both_seqs, 2 * width)
    is_fwd = (lax.broadcasted_iota(jnp.int32, (1, both_seqs, 1), 1) < seqs)
    chosen = jnp.where(is_fwd, projections[:, :, :width], projections[:, :, width:])
    rate_low = chosen[:, :, :rank].astype(jnp.bfloat16).reshape(length * both_seqs, rank)
    step_fwd = jnp.dot(rate_low, dt_weight[ahead], preferred_element_type=jnp.float32)
    step_bwd = jnp.dot(rate_low, dt_weight[back], preferred_element_type=jnp.float32)
    step_fwd = step_fwd.reshape(length, both_seqs, inner) + dt_bias[ahead]
    step_bwd = step_bwd.reshape(length, both_seqs, inner) + dt_bias[back]
    delta = jax.nn.softplus(jnp.where(is_fwd, step_fwd, step_bwd)) * stacked_mask[:, :, None]
    nstate = (width - rank) // 2
    entry = chosen[:, :, rank : rank + nstate]
    readout = chosen[:, :, rank + nstate :]
    return (delta, entry, readout)


def direction_pair(seq_x, seq_mask, ahead, back, proj_weight, dt_weight, dt_bias, a_rate, skip_d,
                   axis):
    length, seqs, inner = seq_x.shape
    stacked_x = jnp.concatenate([seq_x, flipped(seq_x)], axis=1)
    stacked_mask = jnp.concatenate([seq_mask, flipped(seq_mask)], axis=1)
    delta, entry, readout = pair_inputs(
        stacked_x, stacked_mask, ahead, back, proj_weight, dt_weight, dt_bias, seqs
    )
    neg_fwd = -jnp.transpose(a_rate[ahead])
    neg_bwd = -jnp.transpose(a_rate[back])
    neg_rate = jnp.concatenate([rows_of(neg_fwd, seqs), rows_of(neg_bwd, seqs)], axis=1)
    skip = jnp.concatenate([rows_of(skip_d[ahead], seqs), rows_of(skip_d[back], seqs)], axis=0)
    (packed,) = run_scan(stacked_x, delta, entry, readout, neg_rate, skip, None, False, False)
    init_fwd = carried_in(packed[:, :seqs], neg_fwd, axis, False)
    init_bwd = carried_in(packed[:, seqs:], neg_bwd, axis, True)
    init = jnp.concatenate([init_fwd, init_bwd], axis=1)
    y, _ = run_scan(stacked_x, delta, entry, readout, neg_rate, skip, init, False, True)
    return y[:, :seqs] + flipped(y[:, seqs:])


def local(
    tokens,
    tissue,
    ln_gain,
    in_weight,
    conv_weight,
    conv_bias,
    proj_weight,
    dt_weight,
    dt_bias,
    a_rate,
    skip_d,
    out_gain,
    out_weight,
):
    rows_here, cols_here, width = tokens.shape
    inner = in_weight.shape[1] // 2
    normed = layer_norm(tokens.astype(jnp.float32), ln_gain).astype(jnp.bfloat16)
    projected = jnp.dot(
        normed.reshape(rows_here * cols_here, width), in_weight, preferred_element_type=jnp.float32
    )
    projected = projected.astype(jnp.bfloat16).reshape(rows_here, cols_here, 2 * inner)
    inner_part = projected[:, :, :inner]
    gate_part = projected[:, :, inner:]
    padded = padded_2(inner_part, (("row", 0), (("cx", "cz"), 1)), 1)
    conv_out = conv_silu(padded, conv_weight, conv_bias, rows_here, cols_here)
    tissue_wide = tissue.astype(jnp.float32)
    group = lax.axis_size("cz")
    mask_lane = jnp.pad(tissue.astype(jnp.bfloat16), ((0, 0), (0, inner - cols_here)))
    sent = jnp.concatenate([conv_out, mask_lane[:, None, :]], axis=1)
    band = lax.all_to_all(sent, "cz", 0, 1, tiled=True)
    band = band.reshape(rows_here // group, group, cols_here + 1, inner)
    band_x = band[:, :, :cols_here, :].reshape(rows_here // group, group * cols_here, inner)
    band_mask = band[:, :, cols_here, :cols_here].reshape(rows_here // group, group * cols_here)
    conv_t = jnp.transpose(band_x, (1, 0, 2))
    tissue_t = jnp.transpose(band_mask).astype(jnp.float32)
    common = (proj_weight, dt_weight, dt_bias, a_rate, skip_d)
    along_rows = direction_pair(conv_t, tissue_t, 0, 2, *common, "cx")
    along_rows = lax.all_to_all(along_rows, "cz", 0, 1, tiled=True)
    along_cols = direction_pair(conv_out, tissue_wide, 1, 3, *common, "row")
    mixed_sum = jnp.transpose(along_rows, (1, 0, 2)) + along_cols
    mixed = (layer_norm(mixed_sum, out_gain) * jax.nn.silu(gate_part.astype(jnp.float32))).astype(
        jnp.bfloat16
    )
    branch = jnp.dot(
        mixed.reshape(rows_here * cols_here, inner), out_weight, preferred_element_type=jnp.float32
    )
    branch = branch.reshape(rows_here, cols_here, width)
    return (tokens.astype(jnp.float32) + tissue_wide[:, :, None] * branch).astype(jnp.bfloat16)


def solution(mesh):
    cols = mesh.shape["col"]
    group = 8 if cols % 8 == 0 else cols
    grid = mesh.devices.reshape(mesh.shape["row"], cols // group, group)
    mesh = jax.sharding.Mesh(grid, ("row", "cx", "cz"))
    col = ("cx", "cz")
    return jax.shard_map(
        local,
        mesh=mesh,
        in_specs=(
            P("row", col, None),
            P("row", col),
            P(),
            P(),
            P(),
            P(),
            P(),
            P(),
            P(),
            P(),
            P(),
            P(),
            P(),
        ),
        out_specs=P("row", col, None),
        check_vma=False,
    )
```

```python
import functools

import jax
import jax.numpy as jnp
from jax import lax
from jax.experimental import pallas as pl
from jax.sharding import PartitionSpec as P


def padded_2(block, sides, width):
    for axis, dim in sides:
        count = axis_count(axis)
        forward = [(i, i + 1) for i in range(count - 1)]
        backward = [(target, source) for source, target in forward]
        low = lax.ppermute(
            lax.slice_in_dim(block, block.shape[dim] - width, None, axis=dim), axis, forward
        )
        high = lax.ppermute(lax.slice_in_dim(block, 0, width, axis=dim), axis, backward)
        block = jnp.concatenate([low, block, high], axis=dim)
    return block


def axis_count(axis):
    if isinstance(axis, tuple):
        count = 1
        for name in axis:
            count *= lax.axis_size(name)
        return count
    return lax.axis_size(axis)


def layer_norm(values, gain):
    center = values - jnp.mean(values, axis=-1, keepdims=True)
    spread = jnp.mean(center * center, axis=-1, keepdims=True)
    return center * lax.rsqrt(spread + 1e-05) * gain


def conv_silu(padded, conv_weight, conv_bias, height, width):
    summed = jnp.broadcast_to(conv_bias, (height, width, conv_bias.shape[0]))
    for offset_row in range(3):
        for offset_col in range(3):
            window = padded[offset_row : offset_row + height, offset_col : offset_col + width]
            summed = summed + window.astype(jnp.float32) * conv_weight[
                offset_row, offset_col
            ].astype(jnp.float32)
    return jax.nn.silu(summed).astype(jnp.bfloat16)


def scan_kernel(neg_rate_ref, skip_ref, x_ref, delta_ref, entry_ref, readout_ref, *rest,
                length, reverse, with_init, with_y):
    rest = list(rest)
    init_ref = rest.pop(0) if with_init else None
    y_ref = rest.pop(0) if with_y else None
    state_ref = rest.pop(0)
    nstate = neg_rate_ref.shape[0]
    slab = state_ref.shape[1:]
    in_registers = slab[0] <= 8
    if in_registers:
        if with_init:
            start = tuple(init_ref[n] for n in range(nstate))
        else:
            start = tuple(jnp.zeros(slab, jnp.float32) for _ in range(nstate))
    else:
        start = ()
        if with_init:
            state_ref[...] = init_ref[...]
        else:
            state_ref[...] = jnp.zeros(state_ref.shape, state_ref.dtype)

    def step(i, carry):
        summed, states = carry
        t = length - 1 - i if reverse else i
        delta = delta_ref[t]
        x_wide = x_ref[t].astype(jnp.float32)
        drive = delta * x_wide
        entry = entry_ref[t]
        readout = readout_ref[t]
        total = jnp.zeros_like(delta)
        kept = []
        for n in range(nstate):
            before = states[n] if in_registers else state_ref[n]
            state = jnp.exp(delta * neg_rate_ref[n]) * before + drive * entry[:, n : n + 1]
            if in_registers:
                kept.append(state)
            else:
                state_ref[n] = state
            if with_y:
                total = total + readout[:, n : n + 1] * state
        if with_y:
            y_ref[t] = total + skip_ref[...] * x_wide
        return (summed + delta, tuple(kept))

    summed, states = lax.fori_loop(
        0, length, step, (jnp.zeros(slab, jnp.float32), start), unroll=4 if in_registers else 2
    )
    for n, state in enumerate(states):
        state_ref[n] = state
    state_ref[nstate] = summed


def run_scan(seq_x, delta, entry, readout, neg_rate, skip, init, reverse, with_y):
    length, seqs, inner = delta.shape
    nstate = neg_rate.shape[0]
    state_shape = jax.ShapeDtypeStruct((nstate + 1, seqs, inner), jnp.float32)
    out_shape = [state_shape]
    if with_y:
        out_shape = [jax.ShapeDtypeStruct((length, seqs, inner), jnp.float32), state_shape]
    args = [neg_rate, skip, seq_x, delta, entry, readout]
    if init is not None:
        args.append(init)
    kernel = functools.partial(
        scan_kernel, length=length, reverse=reverse, with_init=init is not None, with_y=with_y
    )
    return pl.pallas_call(kernel, out_shape=tuple(out_shape))(*args)


def combine(earlier, later, neg_rate):
    nstate = neg_rate.shape[0]
    decay = jnp.exp(later[nstate][None] * neg_rate[:, None, :])
    state = decay * earlier[:nstate] + later[:nstate]
    return jnp.concatenate([state, (earlier[nstate] + later[nstate])[None]], axis=0)


def carried_in(packed, neg_rate, axis, reverse):
    count = lax.axis_size(axis)
    inclusive = packed
    exclusive = None
    shift = 1
    while shift < count:
        if reverse:
            pairs = [(i + shift, i) for i in range(count - shift)]
        else:
            pairs = [(i, i + shift) for i in range(count - shift)]
        got = lax.ppermute(inclusive, axis, pairs)
        exclusive = got if exclusive is None else combine(got, exclusive, neg_rate)
        if 2 * shift < count:
            inclusive = combine(got, inclusive, neg_rate)
        shift *= 2
    if exclusive is None:
        return jnp.zeros_like(packed)
    return exclusive


def flipped(array):
    return array[::-1]


def rows_of(value, seqs):
    return jnp.broadcast_to(value[..., None, :], value.shape[:-1] + (seqs, value.shape[-1]))


def pair_inputs(stacked_x, stacked_mask, ahead, back, proj_weight, dt_weight, dt_bias, seqs):
    rank = dt_weight.shape[1]
    length, both_seqs, inner = stacked_x.shape
    flat = stacked_x.reshape(length * both_seqs, inner)
    weights = jnp.concatenate([proj_weight[ahead], proj_weight[back]], axis=1)
    width = proj_weight.shape[2]
    projections = jnp.dot(flat, weights, preferred_element_type=jnp.float32)
    projections = projections.reshape(length, both_seqs, 2 * width)
    is_fwd = (lax.broadcasted_iota(jnp.int32, (1, both_seqs, 1), 1) < seqs)
    chosen = jnp.where(is_fwd, projections[:, :, :width], projections[:, :, width:])
    rate_low = chosen[:, :, :rank].astype(jnp.bfloat16).reshape(length * both_seqs, rank)
    step_fwd = jnp.dot(rate_low, dt_weight[ahead], preferred_element_type=jnp.float32)
    step_bwd = jnp.dot(rate_low, dt_weight[back], preferred_element_type=jnp.float32)
    step_fwd = step_fwd.reshape(length, both_seqs, inner) + dt_bias[ahead]
    step_bwd = step_bwd.reshape(length, both_seqs, inner) + dt_bias[back]
    delta = jax.nn.softplus(jnp.where(is_fwd, step_fwd, step_bwd)) * stacked_mask[:, :, None]
    nstate = (width - rank) // 2
    entry = chosen[:, :, rank : rank + nstate]
    readout = chosen[:, :, rank + nstate :]
    return (delta, entry, readout)


def direction_pair(seq_x, seq_mask, ahead, back, proj_weight, dt_weight, dt_bias, a_rate, skip_d,
                   axis):
    _, seqs, _ = seq_x.shape
    stacked_x = jnp.concatenate([seq_x, flipped(seq_x)], axis=1)
    stacked_mask = jnp.concatenate([seq_mask, flipped(seq_mask)], axis=1)
    delta, entry, readout = pair_inputs(
        stacked_x, stacked_mask, ahead, back, proj_weight, dt_weight, dt_bias, seqs
    )
    neg_fwd = -jnp.transpose(a_rate[ahead])
    neg_bwd = -jnp.transpose(a_rate[back])
    neg_rate = jnp.concatenate([rows_of(neg_fwd, seqs), rows_of(neg_bwd, seqs)], axis=1)
    skip = jnp.concatenate([rows_of(skip_d[ahead], seqs), rows_of(skip_d[back], seqs)], axis=0)
    (packed,) = run_scan(stacked_x, delta, entry, readout, neg_rate, skip, None, False, False)
    init_fwd = carried_in(packed[:, :seqs], neg_fwd, axis, False)
    init_bwd = carried_in(packed[:, seqs:], neg_bwd, axis, True)
    init = jnp.concatenate([init_fwd, init_bwd], axis=1)
    y, _ = run_scan(stacked_x, delta, entry, readout, neg_rate, skip, init, False, True)
    return y[:, :seqs] + flipped(y[:, seqs:])


def block(
    tokens,
    tissue,
    ln_gain,
    in_weight,
    conv_weight,
    conv_bias,
    proj_weight,
    dt_weight,
    dt_bias,
    a_rate,
    skip_d,
    out_gain,
    out_weight,
):
    rows_here, cols_here, width = tokens.shape
    inner = in_weight.shape[1] // 2
    normed = layer_norm(tokens.astype(jnp.float32), ln_gain).astype(jnp.bfloat16)
    projected = jnp.dot(
        normed.reshape(rows_here * cols_here, width), in_weight, preferred_element_type=jnp.float32
    )
    projected = projected.astype(jnp.bfloat16).reshape(rows_here, cols_here, 2 * inner)
    inner_part = projected[:, :, :inner]
    gate_part = projected[:, :, inner:]
    padded = padded_2(inner_part, (("row", 0), (("cx", "cz"), 1)), 1)
    conv_out = conv_silu(padded, conv_weight, conv_bias, rows_here, cols_here)
    tissue_wide = tissue.astype(jnp.float32)
    group = lax.axis_size("cz")
    mask_lane = jnp.pad(tissue.astype(jnp.bfloat16), ((0, 0), (0, inner - cols_here)))
    sent = jnp.concatenate([conv_out, mask_lane[:, None, :]], axis=1)
    band = lax.all_to_all(sent, "cz", 0, 1, tiled=True)
    band = band.reshape(rows_here // group, group, cols_here + 1, inner)
    band_x = band[:, :, :cols_here, :].reshape(rows_here // group, group * cols_here, inner)
    band_mask = band[:, :, cols_here, :cols_here].reshape(rows_here // group, group * cols_here)
    conv_t = jnp.transpose(band_x, (1, 0, 2))
    tissue_t = jnp.transpose(band_mask).astype(jnp.float32)
    common = (proj_weight, dt_weight, dt_bias, a_rate, skip_d)
    along_rows = direction_pair(conv_t, tissue_t, 0, 2, *common, "cx")
    along_rows = lax.all_to_all(along_rows, "cz", 0, 1, tiled=True)
    along_cols = direction_pair(conv_out, tissue_wide, 1, 3, *common, "row")
    mixed_sum = jnp.transpose(along_rows, (1, 0, 2)) + along_cols
    mixed = (layer_norm(mixed_sum, out_gain) * jax.nn.silu(gate_part.astype(jnp.float32))).astype(
        jnp.bfloat16
    )
    branch = jnp.dot(
        mixed.reshape(rows_here * cols_here, inner), out_weight, preferred_element_type=jnp.float32
    )
    branch = branch.reshape(rows_here, cols_here, width)
    return (tokens.astype(jnp.float32) + tissue_wide[:, :, None] * branch).astype(jnp.bfloat16)


def solution(mesh):
    cols = mesh.shape["col"]
    group = 8 if cols % 8 == 0 else cols
    grid = mesh.devices.reshape(mesh.shape["row"], cols // group, group)
    mesh = jax.sharding.Mesh(grid, ("row", "cx", "cz"))
    col = ("cx", "cz")
    return jax.shard_map(
        block,
        mesh=mesh,
        in_specs=(
            P("row", col, None),
            P("row", col),
            P(),
            P(),
            P(),
            P(),
            P(),
            P(),
            P(),
            P(),
            P(),
            P(),
            P(),
        ),
        out_specs=P("row", col, None),
        check_vma=False,
    )
```

```python
import functools

import jax
import jax.numpy as jnp
from jax import lax
from jax.experimental import pallas as pl
from jax.sharding import PartitionSpec as P


def padded_2(block, sides, width):
    for axis, dim in sides:
        count = axis_count(axis)
        forward = [(i, i + 1) for i in range(count - 1)]
        backward = [(target, source) for source, target in forward]
        low = lax.ppermute(
            lax.slice_in_dim(block, block.shape[dim] - width, None, axis=dim), axis, forward
        )
        high = lax.ppermute(lax.slice_in_dim(block, 0, width, axis=dim), axis, backward)
        block = jnp.concatenate([low, block, high], axis=dim)
    return block


def axis_count(axis):
    if isinstance(axis, tuple):
        count = 1
        for name in axis:
            count *= lax.axis_size(name)
        return count
    return lax.axis_size(axis)


def layer_norm(values, gain):
    center = values - jnp.mean(values, axis=-1, keepdims=True)
    spread = jnp.mean(center * center, axis=-1, keepdims=True)
    return center * lax.rsqrt(spread + 1e-05) * gain


def conv_silu(padded, conv_weight, conv_bias, height, width):
    summed = jnp.broadcast_to(conv_bias, (height, width, conv_bias.shape[0]))
    for offset_row in range(3):
        for offset_col in range(3):
            window = padded[offset_row : offset_row + height, offset_col : offset_col + width]
            summed = summed + window.astype(jnp.float32) * conv_weight[
                offset_row, offset_col
            ].astype(jnp.float32)
    return jax.nn.silu(summed).astype(jnp.bfloat16)


def direction_inputs(seq_x, seq_mask, proj_one, dtw_one, dtb_one):
    rank = dtw_one.shape[0]
    nstate = (proj_one.shape[1] - rank) // 2
    length, seqs, inner = seq_x.shape
    flat = seq_x.reshape(length * seqs, inner)
    projections = jnp.dot(flat, proj_one, preferred_element_type=jnp.float32)
    rate_low = projections[:, :rank].astype(jnp.bfloat16)
    delta = jax.nn.softplus(
        jnp.dot(rate_low, dtw_one, preferred_element_type=jnp.float32) + dtb_one
    )
    delta = delta.reshape(length, seqs, inner) * seq_mask[:, :, None]
    entry = projections[:, rank : rank + nstate].reshape(length, seqs, nstate)
    readout = projections[:, rank + nstate :].reshape(length, seqs, nstate)
    return (delta, entry, readout)


def scan_kernel(neg_rate_ref, skip_ref, x_ref, delta_ref, entry_ref, readout_ref, *rest,
                length, reverse, with_init, with_y):
    rest = list(rest)
    init_ref = rest.pop(0) if with_init else None
    y_ref = rest.pop(0) if with_y else None
    state_ref = rest.pop(0)
    nstate = neg_rate_ref.shape[0]
    slab = state_ref.shape[1:]
    in_registers = slab[0] <= 8
    if in_registers:
        if with_init:
            start = tuple(init_ref[n] for n in range(nstate))
        else:
            start = tuple(jnp.zeros(slab, jnp.float32) for _ in range(nstate))
    else:
        start = ()
        if with_init:
            state_ref[...] = init_ref[...]
        else:
            state_ref[...] = jnp.zeros(state_ref.shape, state_ref.dtype)

    def step(i, carry):
        summed, states = carry
        t = length - 1 - i if reverse else i
        delta = delta_ref[t]
        x_wide = x_ref[t].astype(jnp.float32)
        drive = delta * x_wide
        entry = entry_ref[t]
        readout = readout_ref[t]
        total = jnp.zeros_like(delta)
        kept = []
        for n in range(nstate):
            before = states[n] if in_registers else state_ref[n]
            state = jnp.exp(delta * neg_rate_ref[n]) * before + drive * entry[:, n : n + 1]
            if in_registers:
                kept.append(state)
            else:
                state_ref[n] = state
            if with_y:
                total = total + readout[:, n : n + 1] * state
        if with_y:
            y_ref[t] = total + skip_ref[...] * x_wide
        return (summed + delta, tuple(kept))

    summed, states = lax.fori_loop(
        0, length, step, (jnp.zeros(slab, jnp.float32), start), unroll=4 if in_registers else 2
    )
    for n, state in enumerate(states):
        state_ref[n] = state
    state_ref[nstate] = summed


def run_scan(seq_x, delta, entry, readout, neg_rate, skip, init, reverse, with_y):
    length, seqs, inner = delta.shape
    nstate = neg_rate.shape[0]
    state_shape = jax.ShapeDtypeStruct((nstate + 1, seqs, inner), jnp.float32)
    out_shape = [state_shape]
    if with_y:
        out_shape = [jax.ShapeDtypeStruct((length, seqs, inner), jnp.float32), state_shape]
    args = [neg_rate, skip, seq_x, delta, entry, readout]
    if init is not None:
        args.append(init)
    kernel = functools.partial(
        scan_kernel, length=length, reverse=reverse, with_init=init is not None, with_y=with_y
    )
    return pl.pallas_call(kernel, out_shape=tuple(out_shape))(*args)


def combine(earlier, later, neg_rate):
    nstate = neg_rate.shape[0]
    decay = jnp.exp(later[nstate][None] * neg_rate[:, None, :])
    state = decay * earlier[:nstate] + later[:nstate]
    return jnp.concatenate([state, (earlier[nstate] + later[nstate])[None]], axis=0)


def pack(message):
    total = message[-1]
    high = total.astype(jnp.bfloat16)
    low = (total - high.astype(jnp.float32)).astype(jnp.bfloat16)
    return jnp.concatenate([message[:-1].astype(jnp.bfloat16), high[None], low[None]], axis=0)


def unpack(message):
    total = message[-2].astype(jnp.float32) + message[-1].astype(jnp.float32)
    return jnp.concatenate([message[:-2].astype(jnp.float32), total[None]], axis=0)


def carried_in(packed, neg_rate, axis, reverse):
    count = lax.axis_size(axis)
    inclusive = packed
    exclusive = None
    shift = 1
    while shift < count:
        if reverse:
            pairs = [(i + shift, i) for i in range(count - shift)]
        else:
            pairs = [(i, i + shift) for i in range(count - shift)]
        if axis == "row":
            got = unpack(lax.ppermute(pack(inclusive), axis, pairs))
        else:
            got = lax.ppermute(inclusive, axis, pairs)
        exclusive = got if exclusive is None else combine(got, exclusive, neg_rate)
        if 2 * shift < count:
            inclusive = combine(got, inclusive, neg_rate)
        shift *= 2
    if exclusive is None:
        return jnp.zeros_like(packed)
    return exclusive


def flipped(array):
    return array[::-1]


def rows_of(value, seqs):
    return jnp.broadcast_to(value[..., None, :], value.shape[:-1] + (seqs, value.shape[-1]))


def pair_inputs(stacked_x, stacked_mask, ahead, back, proj_weight, dt_weight, dt_bias, seqs):
    rank = dt_weight.shape[1]
    length, both_seqs, inner = stacked_x.shape
    flat = stacked_x.reshape(length * both_seqs, inner)
    weights = jnp.concatenate([proj_weight[ahead], proj_weight[back]], axis=1)
    width = proj_weight.shape[2]
    projections = jnp.dot(flat, weights, preferred_element_type=jnp.float32)
    projections = projections.reshape(length, both_seqs, 2 * width)
    is_fwd = (lax.broadcasted_iota(jnp.int32, (1, both_seqs, 1), 1) < seqs)
    chosen = jnp.where(is_fwd, projections[:, :, :width], projections[:, :, width:])
    rate_low = chosen[:, :, :rank].astype(jnp.bfloat16).reshape(length * both_seqs, rank)
    step_fwd = jnp.dot(rate_low, dt_weight[ahead], preferred_element_type=jnp.float32)
    step_bwd = jnp.dot(rate_low, dt_weight[back], preferred_element_type=jnp.float32)
    step_fwd = step_fwd.reshape(length, both_seqs, inner) + dt_bias[ahead]
    step_bwd = step_bwd.reshape(length, both_seqs, inner) + dt_bias[back]
    delta = jax.nn.softplus(jnp.where(is_fwd, step_fwd, step_bwd)) * stacked_mask[:, :, None]
    nstate = (width - rank) // 2
    entry = chosen[:, :, rank : rank + nstate]
    readout = chosen[:, :, rank + nstate :]
    return (delta, entry, readout)


def direction_pair(seq_x, seq_mask, ahead, back, proj_weight, dt_weight, dt_bias, a_rate, skip_d,
                   axis):
    length, seqs, inner = seq_x.shape
    stacked_x = jnp.concatenate([seq_x, flipped(seq_x)], axis=1)
    stacked_mask = jnp.concatenate([seq_mask, flipped(seq_mask)], axis=1)
    delta, entry, readout = pair_inputs(
        stacked_x, stacked_mask, ahead, back, proj_weight, dt_weight, dt_bias, seqs
    )
    neg_fwd = -jnp.transpose(a_rate[ahead])
    neg_bwd = -jnp.transpose(a_rate[back])
    neg_rate = jnp.concatenate([rows_of(neg_fwd, seqs), rows_of(neg_bwd, seqs)], axis=1)
    skip = jnp.concatenate([rows_of(skip_d[ahead], seqs), rows_of(skip_d[back], seqs)], axis=0)
    (packed,) = run_scan(stacked_x, delta, entry, readout, neg_rate, skip, None, False, False)
    init_fwd = carried_in(packed[:, :seqs], neg_fwd, axis, False)
    init_bwd = carried_in(packed[:, seqs:], neg_bwd, axis, True)
    init = jnp.concatenate([init_fwd, init_bwd], axis=1)
    y, _ = run_scan(stacked_x, delta, entry, readout, neg_rate, skip, init, False, True)
    return y[:, :seqs] + flipped(y[:, seqs:])


def local(
    tokens,
    tissue,
    ln_gain,
    in_weight,
    conv_weight,
    conv_bias,
    proj_weight,
    dt_weight,
    dt_bias,
    a_rate,
    skip_d,
    out_gain,
    out_weight,
):
    rows_here, cols_here, width = tokens.shape
    inner = in_weight.shape[1] // 2
    normed = layer_norm(tokens.astype(jnp.float32), ln_gain).astype(jnp.bfloat16)
    projected = jnp.dot(
        normed.reshape(rows_here * cols_here, width), in_weight, preferred_element_type=jnp.float32
    )
    projected = projected.astype(jnp.bfloat16).reshape(rows_here, cols_here, 2 * inner)
    inner_part = projected[:, :, :inner]
    gate_part = projected[:, :, inner:]
    padded = padded_2(inner_part, (("row", 0), (("cx", "cz"), 1)), 1)
    conv_out = conv_silu(padded, conv_weight, conv_bias, rows_here, cols_here)
    tissue_wide = tissue.astype(jnp.float32)
    group = lax.axis_size("cz")
    mask_lane = jnp.pad(tissue.astype(jnp.bfloat16), ((0, 0), (0, inner - cols_here)))
    sent = jnp.concatenate([conv_out, mask_lane[:, None, :]], axis=1)
    band = lax.all_to_all(sent, "cz", 0, 1, tiled=True)
    band = band.reshape(rows_here // group, group, cols_here + 1, inner)
    band_x = band[:, :, :cols_here, :].reshape(rows_here // group, group * cols_here, inner)
    band_mask = band[:, :, cols_here, :cols_here].reshape(rows_here // group, group * cols_here)
    conv_t = jnp.transpose(band_x, (1, 0, 2))
    tissue_t = jnp.transpose(band_mask).astype(jnp.float32)
    common = (proj_weight, dt_weight, dt_bias, a_rate, skip_d)
    along_rows = direction_pair(conv_t, tissue_t, 0, 2, *common, "cx")
    along_rows = lax.all_to_all(along_rows, "cz", 0, 1, tiled=True)
    along_cols = direction_pair(conv_out, tissue_wide, 1, 3, *common, "row")
    mixed_sum = jnp.transpose(along_rows, (1, 0, 2)) + along_cols
    mixed = (layer_norm(mixed_sum, out_gain) * jax.nn.silu(gate_part.astype(jnp.float32))).astype(
        jnp.bfloat16
    )
    branch = jnp.dot(
        mixed.reshape(rows_here * cols_here, inner), out_weight, preferred_element_type=jnp.float32
    )
    branch = branch.reshape(rows_here, cols_here, width)
    return (tokens.astype(jnp.float32) + tissue_wide[:, :, None] * branch).astype(jnp.bfloat16)


def solution(mesh):
    cols = mesh.shape["col"]
    group = 8 if cols % 8 == 0 else cols
    grid = mesh.devices.reshape(mesh.shape["row"], cols // group, group)
    mesh = jax.sharding.Mesh(grid, ("row", "cx", "cz"))
    col = ("cx", "cz")
    return jax.shard_map(
        local,
        mesh=mesh,
        in_specs=(
            P("row", col, None),
            P("row", col),
            P(),
            P(),
            P(),
            P(),
            P(),
            P(),
            P(),
            P(),
            P(),
            P(),
            P(),
        ),
        out_specs=P("row", col, None),
        check_vma=False,
    )
```

```python
import functools

import jax
import jax.numpy as jnp
from jax import lax
from jax.experimental import pallas as pl
from jax.sharding import PartitionSpec as P


def padded_2(block, sides, width):
    for axis, dim in sides:
        count = axis_count(axis)
        forward = [(i, i + 1) for i in range(count - 1)]
        backward = [(target, source) for source, target in forward]
        low = lax.ppermute(
            lax.slice_in_dim(block, block.shape[dim] - width, None, axis=dim), axis, forward
        )
        high = lax.ppermute(lax.slice_in_dim(block, 0, width, axis=dim), axis, backward)
        block = jnp.concatenate([low, block, high], axis=dim)
    return block


def axis_count(axis):
    if isinstance(axis, tuple):
        count = 1
        for name in axis:
            count *= lax.axis_size(name)
        return count
    return lax.axis_size(axis)


def layer_norm(values, gain):
    center = values - jnp.mean(values, axis=-1, keepdims=True)
    spread = jnp.mean(center * center, axis=-1, keepdims=True)
    return center * lax.rsqrt(spread + 1e-05) * gain


def conv_silu(padded, conv_weight, conv_bias, height, width):
    summed = jnp.broadcast_to(conv_bias, (height, width, conv_bias.shape[0]))
    for offset_row in range(3):
        for offset_col in range(3):
            window = padded[offset_row : offset_row + height, offset_col : offset_col + width]
            summed = summed + window.astype(jnp.float32) * conv_weight[
                offset_row, offset_col
            ].astype(jnp.float32)
    return jax.nn.silu(summed).astype(jnp.bfloat16)


def direction_inputs(seq_x, seq_mask, proj_one, dtw_one, dtb_one):
    rank = dtw_one.shape[0]
    nstate = (proj_one.shape[1] - rank) // 2
    length, seqs, inner = seq_x.shape
    flat = seq_x.reshape(length * seqs, inner)
    projections = jnp.dot(flat, proj_one, preferred_element_type=jnp.float32)
    rate_low = projections[:, :rank].astype(jnp.bfloat16)
    delta = jax.nn.softplus(
        jnp.dot(rate_low, dtw_one, preferred_element_type=jnp.float32) + dtb_one
    )
    delta = delta.reshape(length, seqs, inner) * seq_mask[:, :, None]
    entry = projections[:, rank : rank + nstate].reshape(length, seqs, nstate)
    readout = projections[:, rank + nstate :].reshape(length, seqs, nstate)
    return (delta, entry, readout)


def scan_kernel(neg_rate_ref, skip_ref, x_ref, delta_ref, entry_ref, readout_ref, *rest,
                length, reverse, with_init, with_y):
    rest = list(rest)
    init_ref = rest.pop(0) if with_init else None
    y_ref = rest.pop(0) if with_y else None
    state_ref = rest.pop(0)
    nstate = neg_rate_ref.shape[0]
    slab = state_ref.shape[1:]
    in_registers = slab[0] <= 8
    if in_registers:
        if with_init:
            start = tuple(init_ref[n] for n in range(nstate))
        else:
            start = tuple(jnp.zeros(slab, jnp.float32) for _ in range(nstate))
    else:
        start = ()
        if with_init:
            state_ref[...] = init_ref[...]
        else:
            state_ref[...] = jnp.zeros(state_ref.shape, state_ref.dtype)

    def step(i, carry):
        summed, states = carry
        t = length - 1 - i if reverse else i
        delta = delta_ref[t]
        x_wide = x_ref[t].astype(jnp.float32)
        drive = delta * x_wide
        entry = entry_ref[t]
        readout = readout_ref[t]
        total = jnp.zeros_like(delta)
        kept = []
        for n in range(nstate):
            before = states[n] if in_registers else state_ref[n]
            state = jnp.exp(delta * neg_rate_ref[n]) * before + drive * entry[:, n : n + 1]
            if in_registers:
                kept.append(state)
            else:
                state_ref[n] = state
            if with_y:
                total = total + readout[:, n : n + 1] * state
        if with_y:
            y_ref[t] = total + skip_ref[...] * x_wide
        return (summed + delta, tuple(kept))

    summed, states = lax.fori_loop(
        0, length, step, (jnp.zeros(slab, jnp.float32), start), unroll=8 if in_registers else 4
    )
    for n, state in enumerate(states):
        state_ref[n] = state
    state_ref[nstate] = summed


def run_scan(seq_x, delta, entry, readout, neg_rate, skip, init, reverse, with_y):
    length, seqs, inner = delta.shape
    nstate = neg_rate.shape[0]
    state_shape = jax.ShapeDtypeStruct((nstate + 1, seqs, inner), jnp.float32)
    out_shape = [state_shape]
    if with_y:
        out_shape = [jax.ShapeDtypeStruct((length, seqs, inner), jnp.float32), state_shape]
    args = [neg_rate, skip, seq_x, delta, entry, readout]
    if init is not None:
        args.append(init)
    kernel = functools.partial(
        scan_kernel, length=length, reverse=reverse, with_init=init is not None, with_y=with_y
    )
    return pl.pallas_call(kernel, out_shape=tuple(out_shape))(*args)


def combine(earlier, later, neg_rate):
    nstate = neg_rate.shape[0]
    decay = jnp.exp(later[nstate][None] * neg_rate[:, None, :])
    state = decay * earlier[:nstate] + later[:nstate]
    return jnp.concatenate([state, (earlier[nstate] + later[nstate])[None]], axis=0)


def carried_in(packed, neg_rate, axis, reverse):
    count = lax.axis_size(axis)
    inclusive = packed
    exclusive = None
    shift = 1
    while shift < count:
        if reverse:
            pairs = [(i + shift, i) for i in range(count - shift)]
        else:
            pairs = [(i, i + shift) for i in range(count - shift)]
        got = lax.ppermute(inclusive, axis, pairs)
        exclusive = got if exclusive is None else combine(got, exclusive, neg_rate)
        if 2 * shift < count:
            inclusive = combine(got, inclusive, neg_rate)
        shift *= 2
    if exclusive is None:
        return jnp.zeros_like(packed)
    return exclusive


def flipped(array):
    return array[::-1]


def rows_of(value, seqs):
    return jnp.broadcast_to(value[..., None, :], value.shape[:-1] + (seqs, value.shape[-1]))


def pair_inputs(stacked_x, stacked_mask, ahead, back, proj_weight, dt_weight, dt_bias, seqs):
    rank = dt_weight.shape[1]
    length, both_seqs, inner = stacked_x.shape
    flat = stacked_x.reshape(length * both_seqs, inner)
    weights = jnp.concatenate([proj_weight[ahead], proj_weight[back]], axis=1)
    width = proj_weight.shape[2]
    projections = jnp.dot(flat, weights, preferred_element_type=jnp.float32)
    projections = projections.reshape(length, both_seqs, 2 * width)
    is_fwd = (lax.broadcasted_iota(jnp.int32, (1, both_seqs, 1), 1) < seqs)
    chosen = jnp.where(is_fwd, projections[:, :, :width], projections[:, :, width:])
    rate_low = chosen[:, :, :rank].astype(jnp.bfloat16).reshape(length * both_seqs, rank)
    step_fwd = jnp.dot(rate_low, dt_weight[ahead], preferred_element_type=jnp.float32)
    step_bwd = jnp.dot(rate_low, dt_weight[back], preferred_element_type=jnp.float32)
    step_fwd = step_fwd.reshape(length, both_seqs, inner) + dt_bias[ahead]
    step_bwd = step_bwd.reshape(length, both_seqs, inner) + dt_bias[back]
    delta = jax.nn.softplus(jnp.where(is_fwd, step_fwd, step_bwd)) * stacked_mask[:, :, None]
    nstate = (width - rank) // 2
    entry = chosen[:, :, rank : rank + nstate]
    readout = chosen[:, :, rank + nstate :]
    return (delta, entry, readout)


def direction_pair(seq_x, seq_mask, ahead, back, proj_weight, dt_weight, dt_bias, a_rate, skip_d,
                   axis):
    length, seqs, inner = seq_x.shape
    stacked_x = jnp.concatenate([seq_x, flipped(seq_x)], axis=1)
    stacked_mask = jnp.concatenate([seq_mask, flipped(seq_mask)], axis=1)
    delta, entry, readout = pair_inputs(
        stacked_x, stacked_mask, ahead, back, proj_weight, dt_weight, dt_bias, seqs
    )
    neg_fwd = -jnp.transpose(a_rate[ahead])
    neg_bwd = -jnp.transpose(a_rate[back])
    neg_rate = jnp.concatenate([rows_of(neg_fwd, seqs), rows_of(neg_bwd, seqs)], axis=1)
    skip = jnp.concatenate([rows_of(skip_d[ahead], seqs), rows_of(skip_d[back], seqs)], axis=0)
    (packed,) = run_scan(stacked_x, delta, entry, readout, neg_rate, skip, None, False, False)
    init_fwd = carried_in(packed[:, :seqs], neg_fwd, axis, False)
    init_bwd = carried_in(packed[:, seqs:], neg_bwd, axis, True)
    init = jnp.concatenate([init_fwd, init_bwd], axis=1)
    y, _ = run_scan(stacked_x, delta, entry, readout, neg_rate, skip, init, False, True)
    return y[:, :seqs] + flipped(y[:, seqs:])


def local(
    tokens,
    tissue,
    ln_gain,
    in_weight,
    conv_weight,
    conv_bias,
    proj_weight,
    dt_weight,
    dt_bias,
    a_rate,
    skip_d,
    out_gain,
    out_weight,
):
    rows_here, cols_here, width = tokens.shape
    inner = in_weight.shape[1] // 2
    normed = layer_norm(tokens.astype(jnp.float32), ln_gain).astype(jnp.bfloat16)
    projected = jnp.dot(
        normed.reshape(rows_here * cols_here, width), in_weight, preferred_element_type=jnp.float32
    )
    projected = projected.astype(jnp.bfloat16).reshape(rows_here, cols_here, 2 * inner)
    inner_part = projected[:, :, :inner]
    gate_part = projected[:, :, inner:]
    padded = padded_2(inner_part, (("row", 0), (("cx", "cz"), 1)), 1)
    conv_out = conv_silu(padded, conv_weight, conv_bias, rows_here, cols_here)
    tissue_wide = tissue.astype(jnp.float32)
    group = lax.axis_size("cz")
    mask_lane = jnp.pad(tissue.astype(jnp.bfloat16), ((0, 0), (0, inner - cols_here)))
    sent = jnp.concatenate([conv_out, mask_lane[:, None, :]], axis=1)
    band = lax.all_to_all(sent, "cz", 0, 1, tiled=True)
    band = band.reshape(rows_here // group, group, cols_here + 1, inner)
    band_x = band[:, :, :cols_here, :].reshape(rows_here // group, group * cols_here, inner)
    band_mask = band[:, :, cols_here, :cols_here].reshape(rows_here // group, group * cols_here)
    conv_t = jnp.transpose(band_x, (1, 0, 2))
    tissue_t = jnp.transpose(band_mask).astype(jnp.float32)
    common = (proj_weight, dt_weight, dt_bias, a_rate, skip_d)
    along_rows = direction_pair(conv_t, tissue_t, 0, 2, *common, "cx")
    along_rows = lax.all_to_all(along_rows, "cz", 0, 1, tiled=True)
    along_cols = direction_pair(conv_out, tissue_wide, 1, 3, *common, "row")
    mixed_sum = jnp.transpose(along_rows, (1, 0, 2)) + along_cols
    mixed = (layer_norm(mixed_sum, out_gain) * jax.nn.silu(gate_part.astype(jnp.float32))).astype(
        jnp.bfloat16
    )
    branch = jnp.dot(
        mixed.reshape(rows_here * cols_here, inner), out_weight, preferred_element_type=jnp.float32
    )
    branch = branch.reshape(rows_here, cols_here, width)
    return (tokens.astype(jnp.float32) + tissue_wide[:, :, None] * branch).astype(jnp.bfloat16)


def solution(mesh):
    cols = mesh.shape["col"]
    group = 8 if cols % 8 == 0 else cols
    grid = mesh.devices.reshape(mesh.shape["row"], cols // group, group)
    mesh = jax.sharding.Mesh(grid, ("row", "cx", "cz"))
    col = ("cx", "cz")
    return jax.shard_map(
        local,
        mesh=mesh,
        in_specs=(
            P("row", col, None),
            P("row", col),
            P(),
            P(),
            P(),
            P(),
            P(),
            P(),
            P(),
            P(),
            P(),
            P(),
            P(),
        ),
        out_specs=P("row", col, None),
        check_vma=False,
    )
```

```python
import functools

import jax
import jax.numpy as jnp
from jax import lax
from jax.experimental import pallas as pl
from jax.sharding import PartitionSpec as P


def padded_2(block, sides, width):
    for axis, dim in sides:
        count = axis_count(axis)
        forward = [(i, i + 1) for i in range(count - 1)]
        backward = [(target, source) for source, target in forward]
        low = lax.ppermute(
            lax.slice_in_dim(block, block.shape[dim] - width, None, axis=dim), axis, forward
        )
        high = lax.ppermute(lax.slice_in_dim(block, 0, width, axis=dim), axis, backward)
        block = jnp.concatenate([low, block, high], axis=dim)
    return block


def axis_count(axis):
    if isinstance(axis, tuple):
        count = 1
        for name in axis:
            count *= lax.axis_size(name)
        return count
    return lax.axis_size(axis)


def layer_norm(values, gain):
    center = values - jnp.mean(values, axis=-1, keepdims=True)
    spread = jnp.mean(center * center, axis=-1, keepdims=True)
    return center * lax.rsqrt(spread + 1e-05) * gain


def conv_silu(padded, conv_weight, conv_bias, height, width):
    summed = jnp.broadcast_to(conv_bias, (height, width, conv_bias.shape[0]))
    for offset_row in range(3):
        for offset_col in range(3):
            window = padded[offset_row : offset_row + height, offset_col : offset_col + width]
            summed = summed + window.astype(jnp.float32) * conv_weight[
                offset_row, offset_col
            ].astype(jnp.float32)
    return jax.nn.silu(summed).astype(jnp.bfloat16)


def direction_inputs(seq_x, seq_mask, proj_one, dtw_one, dtb_one):
    rank = dtw_one.shape[0]
    nstate = (proj_one.shape[1] - rank) // 2
    length, seqs, inner = seq_x.shape
    flat = seq_x.reshape(length * seqs, inner)
    projections = jnp.dot(flat, proj_one, preferred_element_type=jnp.float32)
    rate_low = projections[:, :rank].astype(jnp.bfloat16)
    delta = jax.nn.softplus(
        jnp.dot(rate_low, dtw_one, preferred_element_type=jnp.float32) + dtb_one
    )
    delta = delta.reshape(length, seqs, inner) * seq_mask[:, :, None]
    entry = projections[:, rank : rank + nstate].reshape(length, seqs, nstate)
    readout = projections[:, rank + nstate :].reshape(length, seqs, nstate)
    return (delta, entry, readout)


def scan_kernel(neg_rate_ref, skip_ref, x_ref, delta_ref, entry_ref, readout_ref, *rest,
                length, reverse, with_init, with_y):
    rest = list(rest)
    init_ref = rest.pop(0) if with_init else None
    y_ref = rest.pop(0) if with_y else None
    state_ref = rest.pop(0)
    nstate = neg_rate_ref.shape[0]
    slab = state_ref.shape[1:]
    in_registers = slab[0] <= 8
    if in_registers:
        if with_init:
            start = tuple(init_ref[n] for n in range(nstate))
        else:
            start = tuple(jnp.zeros(slab, jnp.float32) for _ in range(nstate))
    else:
        start = ()
        if with_init:
            state_ref[...] = init_ref[...]
        else:
            state_ref[...] = jnp.zeros(state_ref.shape, state_ref.dtype)

    def step(i, carry):
        summed, states = carry
        t = length - 1 - i if reverse else i
        delta = delta_ref[t]
        x_wide = x_ref[t].astype(jnp.float32)
        drive = delta * x_wide
        entry = entry_ref[t]
        readout = readout_ref[t]
        total = jnp.zeros_like(delta)
        kept = []
        for n in range(nstate):
            before = states[n] if in_registers else state_ref[n]
            state = jnp.exp(delta * neg_rate_ref[n]) * before + drive * entry[:, n : n + 1]
            if in_registers:
                kept.append(state)
            else:
                state_ref[n] = state
            if with_y:
                total = total + readout[:, n : n + 1] * state
        if with_y:
            y_ref[t] = total + skip_ref[...] * x_wide
        return (summed + delta, tuple(kept))

    summed, states = lax.fori_loop(
        0, length, step, (jnp.zeros(slab, jnp.float32), start), unroll=8
    )
    for n, state in enumerate(states):
        state_ref[n] = state
    state_ref[nstate] = summed


def run_scan(seq_x, delta, entry, readout, neg_rate, skip, init, reverse, with_y):
    length, seqs, inner = delta.shape
    nstate = neg_rate.shape[0]
    state_shape = jax.ShapeDtypeStruct((nstate + 1, seqs, inner), jnp.float32)
    out_shape = [state_shape]
    if with_y:
        out_shape = [jax.ShapeDtypeStruct((length, seqs, inner), jnp.float32), state_shape]
    args = [neg_rate, skip, seq_x, delta, entry, readout]
    if init is not None:
        args.append(init)
    kernel = functools.partial(
        scan_kernel, length=length, reverse=reverse, with_init=init is not None, with_y=with_y
    )
    return pl.pallas_call(kernel, out_shape=tuple(out_shape))(*args)


def combine(earlier, later, neg_rate):
    nstate = neg_rate.shape[0]
    decay = jnp.exp(later[nstate][None] * neg_rate[:, None, :])
    state = decay * earlier[:nstate] + later[:nstate]
    return jnp.concatenate([state, (earlier[nstate] + later[nstate])[None]], axis=0)


def carried_in(packed, neg_rate, axis, reverse):
    count = lax.axis_size(axis)
    inclusive = packed
    exclusive = None
    shift = 1
    while shift < count:
        if reverse:
            pairs = [(i + shift, i) for i in range(count - shift)]
        else:
            pairs = [(i, i + shift) for i in range(count - shift)]
        got = lax.ppermute(inclusive, axis, pairs)
        exclusive = got if exclusive is None else combine(got, exclusive, neg_rate)
        if 2 * shift < count:
            inclusive = combine(got, inclusive, neg_rate)
        shift *= 2
    if exclusive is None:
        return jnp.zeros_like(packed)
    return exclusive


def flipped(array):
    return array[::-1]


def rows_of(value, seqs):
    return jnp.broadcast_to(value[..., None, :], value.shape[:-1] + (seqs, value.shape[-1]))


def pair_inputs(stacked_x, stacked_mask, ahead, back, proj_weight, dt_weight, dt_bias, seqs):
    rank = dt_weight.shape[1]
    length, both_seqs, inner = stacked_x.shape
    flat = stacked_x.reshape(length * both_seqs, inner)
    weights = jnp.concatenate([proj_weight[ahead], proj_weight[back]], axis=1)
    width = proj_weight.shape[2]
    projections = jnp.dot(flat, weights, preferred_element_type=jnp.float32)
    projections = projections.reshape(length, both_seqs, 2 * width)
    is_fwd = (lax.broadcasted_iota(jnp.int32, (1, both_seqs, 1), 1) < seqs)
    chosen = jnp.where(is_fwd, projections[:, :, :width], projections[:, :, width:])
    rate_low = chosen[:, :, :rank].astype(jnp.bfloat16).reshape(length * both_seqs, rank)
    step_fwd = jnp.dot(rate_low, dt_weight[ahead], preferred_element_type=jnp.float32)
    step_bwd = jnp.dot(rate_low, dt_weight[back], preferred_element_type=jnp.float32)
    step_fwd = step_fwd.reshape(length, both_seqs, inner) + dt_bias[ahead]
    step_bwd = step_bwd.reshape(length, both_seqs, inner) + dt_bias[back]
    delta = jax.nn.softplus(jnp.where(is_fwd, step_fwd, step_bwd)) * stacked_mask[:, :, None]
    nstate = (width - rank) // 2
    entry = chosen[:, :, rank : rank + nstate]
    readout = chosen[:, :, rank + nstate :]
    return (delta, entry, readout)


def direction_pair(seq_x, seq_mask, ahead, back, proj_weight, dt_weight, dt_bias, a_rate, skip_d,
                   axis):
    length, seqs, inner = seq_x.shape
    stacked_x = jnp.concatenate([seq_x, flipped(seq_x)], axis=1)
    stacked_mask = jnp.concatenate([seq_mask, flipped(seq_mask)], axis=1)
    delta, entry, readout = pair_inputs(
        stacked_x, stacked_mask, ahead, back, proj_weight, dt_weight, dt_bias, seqs
    )
    neg_fwd = -jnp.transpose(a_rate[ahead])
    neg_bwd = -jnp.transpose(a_rate[back])
    neg_rate = jnp.concatenate([rows_of(neg_fwd, seqs), rows_of(neg_bwd, seqs)], axis=1)
    skip = jnp.concatenate([rows_of(skip_d[ahead], seqs), rows_of(skip_d[back], seqs)], axis=0)
    (packed,) = run_scan(stacked_x, delta, entry, readout, neg_rate, skip, None, False, False)
    init_fwd = carried_in(packed[:, :seqs], neg_fwd, axis, False)
    init_bwd = carried_in(packed[:, seqs:], neg_bwd, axis, True)
    init = jnp.concatenate([init_fwd, init_bwd], axis=1)
    y, _ = run_scan(stacked_x, delta, entry, readout, neg_rate, skip, init, False, True)
    return y[:, :seqs] + flipped(y[:, seqs:])


def local(
    tokens,
    tissue,
    ln_gain,
    in_weight,
    conv_weight,
    conv_bias,
    proj_weight,
    dt_weight,
    dt_bias,
    a_rate,
    skip_d,
    out_gain,
    out_weight,
):
    rows_here, cols_here, width = tokens.shape
    inner = in_weight.shape[1] // 2
    normed = layer_norm(tokens.astype(jnp.float32), ln_gain).astype(jnp.bfloat16)
    projected = jnp.dot(
        normed.reshape(rows_here * cols_here, width), in_weight, preferred_element_type=jnp.float32
    )
    projected = projected.astype(jnp.bfloat16).reshape(rows_here, cols_here, 2 * inner)
    inner_part = projected[:, :, :inner]
    gate_part = projected[:, :, inner:]
    padded = padded_2(inner_part, (("row", 0), (("cx", "cz"), 1)), 1)
    conv_out = conv_silu(padded, conv_weight, conv_bias, rows_here, cols_here)
    tissue_wide = tissue.astype(jnp.float32)
    group = lax.axis_size("cz")
    mask_lane = jnp.pad(tissue.astype(jnp.bfloat16), ((0, 0), (0, inner - cols_here)))
    sent = jnp.concatenate([conv_out, mask_lane[:, None, :]], axis=1)
    band = lax.all_to_all(sent, "cz", 0, 1, tiled=True)
    band = band.reshape(rows_here // group, group, cols_here + 1, inner)
    band_x = band[:, :, :cols_here, :].reshape(rows_here // group, group * cols_here, inner)
    band_mask = band[:, :, cols_here, :cols_here].reshape(rows_here // group, group * cols_here)
    conv_t = jnp.transpose(band_x, (1, 0, 2))
    tissue_t = jnp.transpose(band_mask).astype(jnp.float32)
    common = (proj_weight, dt_weight, dt_bias, a_rate, skip_d)
    along_rows = direction_pair(conv_t, tissue_t, 0, 2, *common, "cx")
    along_rows = lax.all_to_all(along_rows, "cz", 0, 1, tiled=True)
    along_cols = direction_pair(conv_out, tissue_wide, 1, 3, *common, "row")
    mixed_sum = jnp.transpose(along_rows, (1, 0, 2)) + along_cols
    mixed = (layer_norm(mixed_sum, out_gain) * jax.nn.silu(gate_part.astype(jnp.float32))).astype(
        jnp.bfloat16
    )
    branch = jnp.dot(
        mixed.reshape(rows_here * cols_here, inner), out_weight, preferred_element_type=jnp.float32
    )
    branch = branch.reshape(rows_here, cols_here, width)
    return (tokens.astype(jnp.float32) + tissue_wide[:, :, None] * branch).astype(jnp.bfloat16)


def solution(mesh):
    cols = mesh.shape["col"]
    group = 8 if cols % 8 == 0 else cols
    grid = mesh.devices.reshape(mesh.shape["row"], cols // group, group)
    mesh = jax.sharding.Mesh(grid, ("row", "cx", "cz"))
    col = ("cx", "cz")
    return jax.shard_map(
        local,
        mesh=mesh,
        in_specs=(
            P("row", col, None),
            P("row", col),
            P(),
            P(),
            P(),
            P(),
            P(),
            P(),
            P(),
            P(),
            P(),
            P(),
            P(),
        ),
        out_specs=P("row", col, None),
        check_vma=False,
    )
```
